128 devices in a mesh: tm: 32 (over x, z, core), sub: 4 (over y).
Axes of the slice: x: 4, y: 4, z: 4, core: 2. Of those that a mesh axis runs over, the one named last changes fastest.
Arguments:
- vis_coords: float32 [16384, 2, 1024], P(('tm', 'sub')), may hold values from 0 to 31
- vis_values: float32 [16384, 2, 1024], P(('tm', 'sub')), may hold values from -1.6 to 1.6
- block_dest: int32 [16384, 1], P(('tm', 'sub')), may hold values from 0 to 127; in each aligned block of 128 rows (0 to 127, 128 to 255, ...) at most 2 rows name the same one
- block_local: int32 [16384], P(('tm', 'sub')), may hold values from 0 to 15
- block_tile: int32 [16384], P(('tm', 'sub')), may hold values from 0 to 63
- block_counts: int32 [128], P(('tm', 'sub')), may hold values from 64 to 128, as said below
- facet_offsets: int32 [32, 2], replicated, may hold values from 0 to 384
- correction: float32 [32, 128, 128], P('tm', 'sub'), may hold values from 0.2 to 2
Outputs:
- facets: float32 [32, 128, 2, 128], P('tm', 'sub')
The draws below stay inside these ranges and needn't reach their ends.
Inputs may be any that keep to these rules, and one draw needn't show every extreme that they name: `block_dest`: among the 128 blocks of one device at most 2 name the same destination, a bound that some device reaches. `block_counts`: some device's count is 128.
All inputs are finite; a program needn't handle non-finite values.
Results may differ from the reference program's by a relative error of at most 0.000096.
Values sent between devices are 32-bit elements; how exact they have to be, the bound alone decides.
No kernel may reach another device: no remote copies, remote signals or barrier semaphores. Data moves between devices by JAX's collectives and lax.ppermute only.
A program may use at most 128 MiB of HBM per device.

```python
import math
import jax
import jax.numpy as jnp
import numpy as np
from jax import lax

SG = 512
PATCH = 32
FS = 128
VIS = 1024
VB_DEV = 128
SG_PER = 16
CAP = 2
TILES = 64
NB = 16384
NSG = 512
NF = 32
N_TM = 32
N_SUB = 4
DEVICES = 128


def draw_block_counts(key, part):
    first = jax.random.fold_in(key, 11)
    second = jax.random.fold_in(key, 12)
    counts = jax.random.randint(first, (DEVICES,), VB_DEV // 2, VB_DEV + 1)
    chosen = jax.random.randint(second, (), 0, DEVICES)
    counts = jnp.where(jnp.arange(DEVICES) == chosen, VB_DEV, counts)
    return counts.astype(jnp.int32)


def place_ends(drawn, rng, low, largest):
    longest = drawn.shape.index(max(drawn.shape))
    spots = []
    for shift in (0, 1):
        where = [jax.random.randint(jax.random.fold_in(rng, axis), (), 0, length) for axis, length in enumerate(drawn.shape)]
        where[longest] = (where[longest] + shift) % drawn.shape[longest]
        spots.append(tuple(where))
    return drawn.at[spots[0]].set(low).at[spots[1]].set(largest)


def block_scale(stream_key, dims, cuts, low, largest):
    loudness = 1.0
    for position, blocks in cuts:
        steps = jax.random.uniform(jax.random.fold_in(jax.random.fold_in(stream_key, 6), position), (blocks,), jnp.float32, low / len(cuts), largest / len(cuts))
        loudness = loudness * jnp.repeat(jnp.exp(steps), dims[position] // blocks).reshape((-1,) + (1,) * (len(dims) - 1 - position))
    return loudness


def deal_out(key, own, number, rows, number_of, top, limit, lean):
    order = jax.random.permutation(key, number_of)
    crowded, common = shares(number_of, rows * top, limit, lean, True), shares(number_of, rows * top, limit, lean, False)
    places = jnp.arange(number_of)

    def named(sizes, turn):
        used = int((sizes > 0).sum())
        fixed = max(1, used // 4)
        shifted = fixed + (places - fixed + turn * (used - fixed)) % max(1, number_of - fixed)
        return jnp.zeros((number_of,), jnp.int32).at[order[jnp.where(places < fixed, places, shifted)]].set(jnp.asarray(sizes, jnp.int32))

    sizes = jnp.where(number % 4 == 0, named(crowded, number // 4), named(common, number - number // 4 - 1))
    mixed = jax.random.permutation(jax.random.fold_in(own, 3), number_of)
    source_of, taker = mixed[0:number_of // 2 * 2:2], mixed[1:number_of // 2 * 2:2]
    slack = jnp.minimum(sizes[source_of] - 1, limit - sizes[taker]) // 2
    slack = jnp.where((source_of == order[0]) | (taker == order[0]) | (sizes[taker] == 0), 0, jnp.maximum(slack, 0))
    shifted = jax.random.randint(jax.random.fold_in(own, 4), (number_of // 2,), 0, 1 << 20) % (slack + 1)
    sizes = sizes.at[source_of].add(-shifted).at[taker].add(shifted)
    items = jnp.searchsorted(jnp.cumsum(sizes), jnp.arange(rows * top), side="right").astype(jnp.int32)
    listing = items.reshape(top, rows).T
    listing = listing[jax.random.permutation(jax.random.fold_in(own, 1), rows)]
    turn = jax.random.randint(jax.random.fold_in(own, 2), (rows, 1), 0, top)
    return jnp.take_along_axis(listing, (jnp.arange(top)[None, :] + turn) % top, axis=1)


def shares(amount, total, most, lean, full):
    portions = [(1 << 20) // math.isqrt(rank ** lean) + 1 for rank in range(1, amount + 1)]
    largest = most if full else min(most, max(-(-total // amount), total * portions[0] // sum(portions)))
    least = 1 if total - largest >= amount - 1 else 0
    given, rest = [largest] + [least] * (amount - 1), total - largest - least * (amount - 1)
    while rest > 0:
        candidates = [i for i in range(1, amount) if given[i] < largest] or [i for i in range(1, amount) if given[i] < most]
        pool, left = sum([portions[i] for i in candidates]), rest
        for i in candidates:
            addition = min(most - given[i], max(1, left * portions[i] // pool), rest)
            given[i] = given[i] + addition
            rest = rest - addition
    return np.array(given)


def bell_draw(stream_key, dims, width, most, cuts=(), kind=jnp.bfloat16):
    entries = jax.random.normal(stream_key, dims, jnp.float32) * width
    if len(cuts) > 0:
        entries = block_scale(stream_key, dims, cuts, -0.22, 0.18) * entries
    return jnp.clip(entries, min=-most, max=most).astype(kind)


def setup_inputs(seed: int = 0) -> dict:
    key_list = jax.random.split(jax.random.key(seed), 9)
    vis_coords = jnp.clip(31.0 * jax.random.uniform(key_list[0], (NB, 2, VIS), jnp.float32) ** block_scale(key_list[0], (NB, 2, VIS), ((0, 128),), -0.2, 0.2), 0.0, 31.0)
    vis_values = bell_draw(key_list[1], (NB, 2, VIS), 0.2, 1.6, ((0, 128),), jnp.float32)
    block_dest_keys = jax.random.split(jax.random.fold_in(key_list[2], 1), NB // VB_DEV)
    block_dest_turns = jax.random.permutation(jax.random.fold_in(key_list[2], 3), NB // VB_DEV)
    block_dest = jax.vmap(lambda own, number: deal_out(jax.random.fold_in(key_list[2], 2), own, number, VB_DEV, DEVICES, 1, CAP, 2))(block_dest_keys, block_dest_turns).reshape((NB, 1))
    block_local = place_ends(jax.random.randint(key_list[3], (NB,), 0, SG_PER), jax.random.fold_in(key_list[3], 1), 0, SG_PER - 1).astype(jnp.int32)
    block_tile = place_ends(jax.random.randint(key_list[4], (NB,), 0, TILES), jax.random.fold_in(key_list[4], 1), 0, TILES - 1).astype(jnp.int32)
    block_counts = draw_block_counts(jax.random.fold_in(key_list[8], 71), 0)
    facet_offsets = place_ends(jax.random.randint(key_list[6], (NF, 2), 0, SG - FS + 1), jax.random.fold_in(key_list[6], 1), 0, SG - FS).astype(jnp.int32)
    correction = jnp.clip(jnp.exp(math.log(2.0) - 2.3025851 * jax.random.uniform(key_list[7], (NF, FS, FS), jnp.float32) ** block_scale(key_list[7], (NF, FS, FS), ((0, 32), (1, 4)), -0.2, 0.2)), 0.2, 2.0)
    return dict(vis_coords=vis_coords, vis_values=vis_values, block_dest=block_dest, block_local=block_local, block_tile=block_tile, block_counts=block_counts, facet_offsets=facet_offsets, correction=correction)


kernel_width = 0.7

def make_patches(vis_coords, vis_values):
    count = vis_coords.shape[0]
    group = math.gcd(count, 16)
    cells = jnp.arange(PATCH).astype(jnp.float32)

    def one_group(pieces):
        coords, values = pieces
        rows_kernel = jnp.exp(-0.5 * ((coords[:, 0, None, :] - cells[None, :, None]) / kernel_width) ** 2)
        cols_kernel = jnp.exp(-0.5 * ((coords[:, 1, None, :] - cells[None, :, None]) / kernel_width) ** 2)
        weighted = values[:, :, None, :] * cols_kernel[:, None, :, :]
        patch = jnp.einsum('nak,npbk->napb', rows_kernel, weighted, precision=lax.Precision.HIGHEST)
        return patch.reshape(group, 2 * PATCH * PATCH)
    shaped = (vis_coords.reshape(count // group, group, 2, VIS), vis_values.reshape(count // group, group, 2, VIS))
    return lax.map(one_group, shaped).reshape(count, 2 * PATCH * PATCH)

def column_table():
    index = jnp.arange(SG, dtype=jnp.int32)
    phase = index[:, None] * index[None, :] % SG
    angle = phase.astype(jnp.float32) * (2.0 * math.pi / SG)
    scale = 1.0 / math.sqrt(SG)
    cosine = jnp.cos(angle) * scale
    sine = jnp.sin(angle) * scale
    return jnp.concatenate([jnp.concatenate([cosine, -sine], 1), jnp.concatenate([sine, cosine], 1)], 0)

def row_table(first_row, count):
    ys = jnp.arange(SG, dtype=jnp.int32)
    rows = first_row + jnp.arange(count, dtype=jnp.int32)
    phase = ys[:, None] * rows[None, :] % SG
    angle = phase.astype(jnp.float32) * (2.0 * math.pi / SG)
    scale = 1.0 / math.sqrt(SG)
    return jnp.concatenate([jnp.cos(angle) * scale, -jnp.sin(angle) * scale], 1)

def facet_terms(spectrum, table, offsets):
    stride = SG // SG_PER
    total = spectrum[0]
    for local in range(1, SG_PER):
        total = total + jnp.roll(spectrum[local], -local * stride, axis=2)

    def one_facet(offset):
        left = lax.dynamic_slice_in_dim(table, offset[0], FS, 0)
        window = lax.dynamic_slice_in_dim(total, offset[1], FS, 2)
        real_part = window[:, 0]
        imag_part = window[:, 1]
        right = jnp.concatenate([jnp.concatenate([real_part, imag_part], 1), jnp.concatenate([-imag_part, real_part], 1)], 0)
        return jnp.dot(left, right, precision=lax.Precision.HIGHEST)
    return lax.map(one_facet, offsets)

def reference(vis_coords, vis_values, block_dest, block_local, block_tile, block_counts, facet_offsets, correction):
    patches = make_patches(vis_coords, vis_values)
    slots = jnp.arange(NB, dtype=jnp.int32)
    live_block = slots % VB_DEV < block_counts[slots // VB_DEV]
    target = block_dest[:, 0]
    col_tiles = SG // PATCH
    band_tiles = SG // N_SUB // PATCH
    subgrid = target // N_SUB * SG_PER + block_local
    row_tile = target % N_SUB * band_tiles + block_tile // col_tiles
    col_tile = block_tile % col_tiles
    tile_id = (subgrid * col_tiles + row_tile) * col_tiles + col_tile
    tile_id = jnp.where(live_block, tile_id, NSG * col_tiles * col_tiles).astype(jnp.int32)
    tiles = jax.ops.segment_sum(patches, tile_id, num_segments=NSG * col_tiles * col_tiles + 1)[:-1]
    grid = tiles.reshape(NSG, col_tiles, col_tiles, PATCH, 2, PATCH).transpose(0, 1, 3, 4, 2, 5).reshape(NSG * SG, 2 * SG)
    spectrum = jnp.dot(grid, column_table(), precision=lax.Precision.HIGHEST).reshape(N_TM, SG_PER, SG, 2, SG)
    spectrum = lax.optimization_barrier(jnp.sum(spectrum, axis=0))
    table = row_table(jnp.int32(0), SG)
    terms = facet_terms(spectrum, table, facet_offsets)
    return terms.reshape(NF, FS, 2, FS) * correction[:, :, None, :]
```

```python
import math

import jax
import jax.numpy as jnp
from jax import lax
from jax.sharding import PartitionSpec as P

SG = 512
PATCH = 32
FS = 128
VIS = 1024
SG_PER = 16


kernel_width = 0.7


def make_phased_patches(vis_coords, vis_values, live, local):
    count = vis_coords.shape[0]
    cells = jnp.arange(PATCH, dtype=jnp.float32)
    rows_kernel = jnp.exp(
        -0.5 * ((vis_coords[:, 0, None, :] - cells[None, :, None]) / kernel_width) ** 2
    )
    cols_kernel = jnp.exp(
        -0.5 * ((vis_coords[:, 1, None, :] - cells[None, :, None]) / kernel_width) ** 2
    )
    values = jnp.where(live[:, None, None], vis_values, 0.0)
    phase = (jnp.arange(PATCH, dtype=jnp.int32)[None, :] * local[:, None]) % SG_PER
    angle = phase.astype(jnp.float32) * (2.0 * math.pi / SG_PER)
    cos_b = jnp.cos(angle)[:, :, None]
    sin_b = jnp.sin(angle)[:, :, None]
    v_re = values[:, 0, None, :]
    v_im = values[:, 1, None, :]
    w_re = cols_kernel * (v_re * cos_b + v_im * sin_b)
    w_im = cols_kernel * (v_im * cos_b - v_re * sin_b)
    weighted = jnp.stack([w_re, w_im], axis=1)
    patch = jnp.einsum("nak,npbk->napb", rows_kernel, weighted, precision=lax.Precision.HIGHEST)
    return patch.reshape(count, 2 * PATCH * PATCH)


def column_table():
    index = jnp.arange(SG, dtype=jnp.int32)
    phase = index[:, None] * index[None, :] % SG
    angle = phase.astype(jnp.float32) * (2.0 * math.pi / SG)
    scale = 1.0 / math.sqrt(SG)
    cosine = jnp.cos(angle) * scale
    sine = jnp.sin(angle) * scale
    return jnp.concatenate(
        [jnp.concatenate([cosine, -sine], 1), jnp.concatenate([sine, cosine], 1)], 0
    )


def body(
    vis_coords,
    vis_values,
    block_dest,
    block_local,
    block_tile,
    block_counts,
    facet_offsets,
    correction,
):
    n_tm = lax.axis_size("tm")
    n_sub = lax.axis_size("sub")
    devices = n_tm * n_sub
    blocks = vis_coords.shape[0]
    band_rows = SG // n_sub
    band_tiles = band_rows // PATCH
    col_tiles = SG // PATCH
    tiles_all = col_tiles * col_tiles
    chunk = SG // devices
    facet_rows = FS // n_sub

    live = jnp.arange(blocks, dtype=jnp.int32) < block_counts[0]
    patches = make_phased_patches(vis_coords, vis_values, live, block_local)

    target = block_dest[:, 0]
    row_tile = (target % n_sub) * band_tiles + block_tile // col_tiles
    tile_id = row_tile * col_tiles + block_tile % col_tiles
    placer = (
        tile_id[None, :] == jnp.arange(tiles_all, dtype=jnp.int32)[:, None]
    ).astype(jnp.float32)
    tiles = jnp.dot(placer, patches, precision=lax.Precision.HIGHEST)
    per_tile_row = PATCH // chunk
    outgoing = (
        tiles.reshape(col_tiles, col_tiles, per_tile_row, chunk, 2, PATCH)
        .transpose(0, 2, 3, 4, 1, 5)
        .reshape(devices, chunk, 2, SG)
    )
    arrived = lax.all_to_all(
        outgoing, ("tm", "sub"), split_axis=0, concat_axis=0, tiled=True
    )
    grid_rows = jnp.sum(arrived, axis=0).reshape(chunk, 2 * SG)
    spectrum = jnp.dot(grid_rows, column_table(), precision=lax.Precision.HIGHEST).reshape(
        chunk, 2, SG
    )

    offsets = jnp.clip(facet_offsets, 0, SG - FS)
    dest_facet = jnp.arange(devices, dtype=jnp.int32) // n_sub
    columns = offsets[dest_facet, 1][:, None] + jnp.arange(FS, dtype=jnp.int32)[None, :]
    windows = jnp.take(spectrum, columns.reshape(-1), axis=2)
    windows = windows.reshape(chunk, 2, devices, FS).transpose(2, 0, 1, 3)
    gathered = lax.all_to_all(
        windows, ("tm", "sub"), split_axis=0, concat_axis=0, tiled=True
    ).reshape(SG, 2, FS)

    facet = lax.axis_index("tm")
    band = lax.axis_index("sub")
    first_y = offsets[facet, 0] + band * facet_rows
    ys = first_y + jnp.arange(facet_rows, dtype=jnp.int32)
    rs = jnp.arange(SG, dtype=jnp.int32)
    angle = ((ys[:, None] * rs[None, :]) % SG).astype(jnp.float32) * (2.0 * math.pi / SG)
    scale = 1.0 / math.sqrt(SG)
    left = jnp.concatenate([jnp.cos(angle) * scale, jnp.sin(angle) * scale], 1)
    real_part = gathered[:, 0]
    imag_part = gathered[:, 1]
    right = jnp.concatenate(
        [
            jnp.concatenate([real_part, imag_part], 1),
            jnp.concatenate([imag_part, -real_part], 1),
        ],
        0,
    )
    summed = jnp.dot(left, right, precision=lax.Precision.HIGHEST).reshape(
        1, facet_rows, 2, FS
    )
    return summed * correction[:, :, None, :]


def solution(mesh):
    in_specs = (
        P(("tm", "sub"), None, None),
        P(("tm", "sub"), None, None),
        P(("tm", "sub"), None),
        P(("tm", "sub")),
        P(("tm", "sub")),
        P(("tm", "sub")),
        P(),
        P("tm", "sub", None),
    )
    out_specs = P("tm", "sub", None, None)
    return jax.shard_map(body, mesh=mesh, in_specs=in_specs, out_specs=out_specs, check_vma=False)
```

```python
import math

import jax
import jax.numpy as jnp
from jax import lax
from jax.sharding import PartitionSpec as P

SG = 512
PATCH = 32
FS = 128
VIS = 1024
SG_PER = 16


kernel_width = 0.7


def make_phased_patches(vis_coords, vis_values, live, local):
    count = vis_coords.shape[0]
    cells = jnp.arange(PATCH, dtype=jnp.float32)
    rows_kernel = jnp.exp(
        -0.5 * ((vis_coords[:, 0, None, :] - cells[None, :, None]) / kernel_width) ** 2
    )
    cols_kernel = jnp.exp(
        -0.5 * ((vis_coords[:, 1, None, :] - cells[None, :, None]) / kernel_width) ** 2
    )
    values = jnp.where(live[:, None, None], vis_values, 0.0)
    phase = (jnp.arange(PATCH, dtype=jnp.int32)[None, :] * local[:, None]) % SG_PER
    angle = phase.astype(jnp.float32) * (2.0 * math.pi / SG_PER)
    cos_b = jnp.cos(angle)[:, :, None]
    sin_b = jnp.sin(angle)[:, :, None]
    v_re = values[:, 0, None, :]
    v_im = values[:, 1, None, :]
    w_re = cols_kernel * (v_re * cos_b + v_im * sin_b)
    w_im = cols_kernel * (v_im * cos_b - v_re * sin_b)
    weighted = jnp.stack([w_re, w_im], axis=1)
    patch = jnp.einsum("nak,npbk->napb", rows_kernel, weighted, precision=lax.Precision.HIGHEST)
    return patch.reshape(count, 2 * PATCH * PATCH)


def column_table():
    index = jnp.arange(SG, dtype=jnp.int32)
    phase = index[:, None] * index[None, :] % SG
    angle = phase.astype(jnp.float32) * (2.0 * math.pi / SG)
    scale = 1.0 / math.sqrt(SG)
    cosine = jnp.cos(angle) * scale
    sine = jnp.sin(angle) * scale
    return jnp.concatenate(
        [jnp.concatenate([cosine, -sine], 1), jnp.concatenate([sine, cosine], 1)], 0
    )


def body(
    vis_coords,
    vis_values,
    block_dest,
    block_local,
    block_tile,
    block_counts,
    facet_offsets,
    correction,
):
    n_tm = lax.axis_size("tm")
    n_sub = lax.axis_size("sub")
    devices = n_tm * n_sub
    blocks = vis_coords.shape[0]
    band_rows = SG // n_sub
    band_tiles = band_rows // PATCH
    col_tiles = SG // PATCH
    tiles_all = col_tiles * col_tiles
    chunk = SG // devices
    facet_rows = FS // n_sub

    live = jnp.arange(blocks, dtype=jnp.int32) < block_counts[0]
    patches = make_phased_patches(vis_coords, vis_values, live, block_local)

    target = block_dest[:, 0]
    row_tile = (target % n_sub) * band_tiles + block_tile // col_tiles
    tile_id = row_tile * col_tiles + block_tile % col_tiles
    placer = (
        tile_id[None, :] == jnp.arange(tiles_all, dtype=jnp.int32)[:, None]
    ).astype(jnp.float32)
    tiles = jnp.dot(placer, patches, precision=lax.Precision.HIGHEST)
    per_tile_row = PATCH // chunk
    outgoing = (
        tiles.reshape(col_tiles, col_tiles, per_tile_row, chunk, 2, PATCH)
        .transpose(0, 2, 3, 4, 1, 5)
        .reshape(devices, chunk, 2, SG)
    )
    arrived = lax.all_to_all(
        outgoing, ("tm", "sub"), split_axis=0, concat_axis=0, tiled=True
    )
    grid_rows = jnp.sum(arrived, axis=0).reshape(chunk, 2 * SG)
    spectrum = jnp.dot(grid_rows, column_table(), precision=lax.Precision.HIGHEST).reshape(
        chunk, 2, SG
    )

    offsets = jnp.clip(facet_offsets, 0, SG - FS)
    windows = jax.vmap(lambda start: lax.dynamic_slice_in_dim(spectrum, start, FS, 2))(
        offsets[:, 1]
    )
    windows = jnp.broadcast_to(
        windows[:, None], (n_tm, n_sub, chunk, 2, FS)
    ).reshape(devices, chunk, 2, FS)
    gathered = lax.all_to_all(
        windows, ("tm", "sub"), split_axis=0, concat_axis=0, tiled=True
    ).reshape(SG, 2, FS)

    facet = lax.axis_index("tm")
    band = lax.axis_index("sub")
    first_y = offsets[facet, 0] + band * facet_rows
    ys = first_y + jnp.arange(facet_rows, dtype=jnp.int32)
    rs = jnp.arange(SG, dtype=jnp.int32)
    angle = ((ys[:, None] * rs[None, :]) % SG).astype(jnp.float32) * (2.0 * math.pi / SG)
    scale = 1.0 / math.sqrt(SG)
    left = jnp.concatenate([jnp.cos(angle) * scale, jnp.sin(angle) * scale], 1)
    real_part = gathered[:, 0]
    imag_part = gathered[:, 1]
    right = jnp.concatenate(
        [
            jnp.concatenate([real_part, imag_part], 1),
            jnp.concatenate([imag_part, -real_part], 1),
        ],
        0,
    )
    summed = jnp.dot(left, right, precision=lax.Precision.HIGHEST).reshape(
        1, facet_rows, 2, FS
    )
    return summed * correction[:, :, None, :]


def solution(mesh):
    in_specs = (
        P(("tm", "sub"), None, None),
        P(("tm", "sub"), None, None),
        P(("tm", "sub"), None),
        P(("tm", "sub")),
        P(("tm", "sub")),
        P(("tm", "sub")),
        P(),
        P("tm", "sub", None),
    )
    out_specs = P("tm", "sub", None, None)
    return jax.shard_map(body, mesh=mesh, in_specs=in_specs, out_specs=out_specs, check_vma=False)
```

```python
import math

import jax
import jax.numpy as jnp
from jax import lax
from jax.experimental import pallas as pl
from jax.sharding import PartitionSpec as P

SG = 512
PATCH = 32
FS = 128
VIS = 1024
SG_PER = 16


kernel_width = 0.7


def patch_kernel(coords_ref, values_ref, phase_ref, out_ref):
    cells = lax.broadcasted_iota(jnp.int32, (PATCH, 1), 0).astype(jnp.float32)

    def one_block(i, carry):
        x = coords_ref[i, 0:1, :]
        y = coords_ref[i, 1:2, :]
        rows_kernel = jnp.exp(-0.5 * ((x - cells) / kernel_width) ** 2)
        cols_kernel = jnp.exp(-0.5 * ((y - cells) / kernel_width) ** 2)
        v_re = values_ref[i, 0:1, :]
        v_im = values_ref[i, 1:2, :]
        cos_b = phase_ref[i, 0]
        sin_b = phase_ref[i, 1]
        w_re = cols_kernel * (v_re * cos_b + v_im * sin_b)
        w_im = cols_kernel * (v_im * cos_b - v_re * sin_b)
        weighted = jnp.concatenate([w_re, w_im], axis=0)
        out_ref[i] = lax.dot_general(
            rows_kernel,
            weighted,
            (((1,), (1,)), ((), ())),
            precision=lax.Precision.HIGHEST,
            preferred_element_type=jnp.float32,
        )
        return carry

    lax.fori_loop(0, out_ref.shape[0], one_block, 0)


def make_phased_patches(vis_coords, vis_values, live, local):
    count = vis_coords.shape[0]
    step = 8
    phase = (jnp.arange(PATCH, dtype=jnp.int32)[None, :] * local[:, None]) % SG_PER
    angle = phase.astype(jnp.float32) * (2.0 * math.pi / SG_PER)
    keep = live.astype(jnp.float32)[:, None]
    phases = jnp.stack([jnp.cos(angle) * keep, jnp.sin(angle) * keep], axis=1)[..., None]
    spec = pl.BlockSpec((step, 2, VIS), lambda i: (i, 0, 0))
    patch = pl.pallas_call(
        patch_kernel,
        grid=(count // step,),
        in_specs=[spec, spec, pl.BlockSpec((step, 2, PATCH, 1), lambda i: (i, 0, 0, 0))],
        out_specs=pl.BlockSpec((step, PATCH, 2 * PATCH), lambda i: (i, 0, 0)),
        out_shape=jax.ShapeDtypeStruct((count, PATCH, 2 * PATCH), jnp.float32),
        cost_estimate=pl.CostEstimate(
            flops=count * PATCH * 2 * PATCH * VIS * 2,
            transcendentals=count * 2 * PATCH * VIS,
            bytes_accessed=count * (4 * VIS + 2 * PATCH * PATCH) * 4,
        ),
    )(vis_coords, vis_values, phases)
    return patch.reshape(count, 2 * PATCH * PATCH)


def column_table():
    index = jnp.arange(SG, dtype=jnp.int32)
    phase = index[:, None] * index[None, :] % SG
    angle = phase.astype(jnp.float32) * (2.0 * math.pi / SG)
    scale = 1.0 / math.sqrt(SG)
    cosine = jnp.cos(angle) * scale
    sine = jnp.sin(angle) * scale
    return jnp.concatenate(
        [jnp.concatenate([cosine, -sine], 1), jnp.concatenate([sine, cosine], 1)], 0
    )


def body(
    vis_coords,
    vis_values,
    block_dest,
    block_local,
    block_tile,
    block_counts,
    facet_offsets,
    correction,
):
    n_tm = lax.axis_size("tm")
    n_sub = lax.axis_size("sub")
    devices = n_tm * n_sub
    blocks = vis_coords.shape[0]
    band_rows = SG // n_sub
    band_tiles = band_rows // PATCH
    col_tiles = SG // PATCH
    tiles_all = col_tiles * col_tiles
    chunk = SG // devices
    facet_rows = FS // n_sub

    live = jnp.arange(blocks, dtype=jnp.int32) < block_counts[0]
    patches = make_phased_patches(vis_coords, vis_values, live, block_local)

    target = block_dest[:, 0]
    row_tile = (target % n_sub) * band_tiles + block_tile // col_tiles
    tile_id = row_tile * col_tiles + block_tile % col_tiles
    placer = (
        tile_id[None, :] == jnp.arange(tiles_all, dtype=jnp.int32)[:, None]
    ).astype(jnp.float32)
    tiles = jnp.dot(placer, patches, precision=lax.Precision.HIGHEST)
    per_tile_row = PATCH // chunk
    outgoing = (
        tiles.reshape(col_tiles, col_tiles, per_tile_row, chunk, 2, PATCH)
        .transpose(0, 2, 3, 4, 1, 5)
        .reshape(devices, chunk, 2, SG)
    )
    arrived = lax.all_to_all(
        outgoing, ("tm", "sub"), split_axis=0, concat_axis=0, tiled=True
    )
    grid_rows = jnp.sum(arrived, axis=0).reshape(chunk, 2 * SG)
    spectrum = jnp.dot(grid_rows, column_table(), precision=lax.Precision.HIGHEST).reshape(
        chunk, 2, SG
    )

    offsets = jnp.clip(facet_offsets, 0, SG - FS)
    windows = jax.vmap(lambda start: lax.dynamic_slice_in_dim(spectrum, start, FS, 2))(
        offsets[:, 1]
    )
    windows = jnp.broadcast_to(
        windows[:, None], (n_tm, n_sub, chunk, 2, FS)
    ).reshape(devices, chunk, 2, FS)
    gathered = lax.all_to_all(
        windows, ("tm", "sub"), split_axis=0, concat_axis=0, tiled=True
    ).reshape(SG, 2, FS)

    facet = lax.axis_index("tm")
    band = lax.axis_index("sub")
    first_y = offsets[facet, 0] + band * facet_rows
    ys = first_y + jnp.arange(facet_rows, dtype=jnp.int32)
    rs = jnp.arange(SG, dtype=jnp.int32)
    angle = ((ys[:, None] * rs[None, :]) % SG).astype(jnp.float32) * (2.0 * math.pi / SG)
    scale = 1.0 / math.sqrt(SG)
    left = jnp.concatenate([jnp.cos(angle) * scale, jnp.sin(angle) * scale], 1)
    real_part = gathered[:, 0]
    imag_part = gathered[:, 1]
    right = jnp.concatenate(
        [
            jnp.concatenate([real_part, imag_part], 1),
            jnp.concatenate([imag_part, -real_part], 1),
        ],
        0,
    )
    summed = jnp.dot(left, right, precision=lax.Precision.HIGHEST).reshape(
        1, facet_rows, 2, FS
    )
    return summed * correction[:, :, None, :]


def solution(mesh):
    in_specs = (
        P(("tm", "sub"), None, None),
        P(("tm", "sub"), None, None),
        P(("tm", "sub"), None),
        P(("tm", "sub")),
        P(("tm", "sub")),
        P(("tm", "sub")),
        P(),
        P("tm", "sub", None),
    )
    out_specs = P("tm", "sub", None, None)
    return jax.shard_map(body, mesh=mesh, in_specs=in_specs, out_specs=out_specs, check_vma=False)
```

```python
import math

import jax
import jax.numpy as jnp
from jax import lax
from jax.experimental import pallas as pl
from jax.sharding import PartitionSpec as P

SG = 512
PATCH = 32
FS = 128
VIS = 1024
SG_PER = 16


kernel_width = 0.7


def split_bf16(x):
    high = x.astype(jnp.bfloat16)
    low = (x - high.astype(jnp.float32)).astype(jnp.bfloat16)
    return jnp.concatenate([high, low], axis=0)


def patch_kernel(coords_ref, values_ref, phase_ref, out_ref):
    cells = lax.broadcasted_iota(jnp.int32, (PATCH, 1), 0).astype(jnp.float32)

    def one_block(i, carry):
        x = coords_ref[i, 0:1, :]
        y = coords_ref[i, 1:2, :]
        rows_kernel = jnp.exp(-0.5 * ((x - cells) / kernel_width) ** 2)
        cols_kernel = jnp.exp(-0.5 * ((y - cells) / kernel_width) ** 2)
        weighted = jnp.concatenate(
            [cols_kernel * values_ref[i, 0:1, :], cols_kernel * values_ref[i, 1:2, :]], axis=0
        )
        both = lax.dot_general(
            split_bf16(rows_kernel),
            split_bf16(weighted),
            (((1,), (1,)), ((), ())),
            preferred_element_type=jnp.float32,
        )
        width = 2 * PATCH
        plain = (both[:PATCH, :width] + both[:PATCH, width:]) + (
            both[PATCH:, :width] + both[PATCH:, width:]
        )
        real_part = plain[:, :PATCH]
        imag_part = plain[:, PATCH:]
        phase = phase_ref[pl.ds(i, 1), :]
        cos_b = phase[:, :PATCH]
        sin_b = phase[:, PATCH:]
        out_ref[i] = jnp.concatenate(
            [real_part * cos_b + imag_part * sin_b, imag_part * cos_b - real_part * sin_b],
            axis=1,
        )
        return carry

    lax.fori_loop(0, out_ref.shape[0], one_block, 0)


def make_phased_patches(vis_coords, vis_values, live, local):
    count = vis_coords.shape[0]
    step = 8
    phase = (jnp.arange(PATCH, dtype=jnp.int32)[None, :] * local[:, None]) % SG_PER
    angle = phase.astype(jnp.float32) * (2.0 * math.pi / SG_PER)
    keep = live.astype(jnp.float32)[:, None]
    phases = jnp.concatenate([jnp.cos(angle) * keep, jnp.sin(angle) * keep], axis=1)
    spec = pl.BlockSpec((step, 2, VIS), lambda i: (i, 0, 0))
    patch = pl.pallas_call(
        patch_kernel,
        grid=(count // step,),
        in_specs=[spec, spec, pl.BlockSpec((step, 2 * PATCH), lambda i: (i, 0))],
        out_specs=pl.BlockSpec((step, PATCH, 2 * PATCH), lambda i: (i, 0, 0)),
        out_shape=jax.ShapeDtypeStruct((count, PATCH, 2 * PATCH), jnp.float32),
        cost_estimate=pl.CostEstimate(
            flops=count * 4 * PATCH * 4 * PATCH * VIS * 2,
            transcendentals=count * 2 * PATCH * VIS,
            bytes_accessed=count * (4 * VIS + 2 * PATCH * PATCH) * 4,
        ),
    )(vis_coords, vis_values, phases)
    return patch.reshape(count, 2 * PATCH * PATCH)


def column_table():
    index = jnp.arange(SG, dtype=jnp.int32)
    phase = index[:, None] * index[None, :] % SG
    angle = phase.astype(jnp.float32) * (2.0 * math.pi / SG)
    scale = 1.0 / math.sqrt(SG)
    cosine = jnp.cos(angle) * scale
    sine = jnp.sin(angle) * scale
    return jnp.concatenate(
        [jnp.concatenate([cosine, -sine], 1), jnp.concatenate([sine, cosine], 1)], 0
    )


def body(
    vis_coords,
    vis_values,
    block_dest,
    block_local,
    block_tile,
    block_counts,
    facet_offsets,
    correction,
):
    n_tm = lax.axis_size("tm")
    n_sub = lax.axis_size("sub")
    devices = n_tm * n_sub
    blocks = vis_coords.shape[0]
    band_rows = SG // n_sub
    band_tiles = band_rows // PATCH
    col_tiles = SG // PATCH
    tiles_all = col_tiles * col_tiles
    chunk = SG // devices
    facet_rows = FS // n_sub

    live = jnp.arange(blocks, dtype=jnp.int32) < block_counts[0]
    patches = make_phased_patches(vis_coords, vis_values, live, block_local)

    target = block_dest[:, 0]
    row_tile = (target % n_sub) * band_tiles + block_tile // col_tiles
    tile_id = row_tile * col_tiles + block_tile % col_tiles
    placer = (
        tile_id[None, :] == jnp.arange(tiles_all, dtype=jnp.int32)[:, None]
    ).astype(jnp.float32)
    tiles = jnp.dot(placer, patches, precision=lax.Precision.HIGHEST)
    per_tile_row = PATCH // chunk
    outgoing = (
        tiles.reshape(col_tiles, col_tiles, per_tile_row, chunk, 2, PATCH)
        .transpose(0, 2, 3, 4, 1, 5)
        .reshape(devices, chunk, 2, SG)
    )
    arrived = lax.all_to_all(
        outgoing, ("tm", "sub"), split_axis=0, concat_axis=0, tiled=True
    )
    grid_rows = jnp.sum(arrived, axis=0).reshape(chunk, 2 * SG)
    spectrum = jnp.dot(grid_rows, column_table(), precision=lax.Precision.HIGHEST).reshape(
        chunk, 2, SG
    )

    offsets = jnp.clip(facet_offsets, 0, SG - FS)
    windows = jax.vmap(lambda start: lax.dynamic_slice_in_dim(spectrum, start, FS, 2))(
        offsets[:, 1]
    )
    windows = jnp.broadcast_to(
        windows[:, None], (n_tm, n_sub, chunk, 2, FS)
    ).reshape(devices, chunk, 2, FS)
    gathered = lax.all_to_all(
        windows, ("tm", "sub"), split_axis=0, concat_axis=0, tiled=True
    ).reshape(SG, 2, FS)

    facet = lax.axis_index("tm")
    band = lax.axis_index("sub")
    first_y = offsets[facet, 0] + band * facet_rows
    ys = first_y + jnp.arange(facet_rows, dtype=jnp.int32)
    rs = jnp.arange(SG, dtype=jnp.int32)
    angle = ((ys[:, None] * rs[None, :]) % SG).astype(jnp.float32) * (2.0 * math.pi / SG)
    scale = 1.0 / math.sqrt(SG)
    left = jnp.concatenate([jnp.cos(angle) * scale, jnp.sin(angle) * scale], 1)
    real_part = gathered[:, 0]
    imag_part = gathered[:, 1]
    right = jnp.concatenate(
        [
            jnp.concatenate([real_part, imag_part], 1),
            jnp.concatenate([imag_part, -real_part], 1),
        ],
        0,
    )
    summed = jnp.dot(left, right, precision=lax.Precision.HIGHEST).reshape(
        1, facet_rows, 2, FS
    )
    return summed * correction[:, :, None, :]


def solution(mesh):
    in_specs = (
        P(("tm", "sub"), None, None),
        P(("tm", "sub"), None, None),
        P(("tm", "sub"), None),
        P(("tm", "sub")),
        P(("tm", "sub")),
        P(("tm", "sub")),
        P(),
        P("tm", "sub", None),
    )
    out_specs = P("tm", "sub", None, None)
    return jax.shard_map(body, mesh=mesh, in_specs=in_specs, out_specs=out_specs, check_vma=False)
```

```python
import math

import jax
import jax.numpy as jnp
from jax import lax
from jax.experimental import pallas as pl
from jax.sharding import PartitionSpec as P

SG = 512
PATCH = 32
FS = 128
VIS = 1024
SG_PER = 16


kernel_width = 0.7
gauss_scale = -0.5 / (kernel_width * kernel_width) / math.log(2.0)


def split_bf16(x):
    high = x.astype(jnp.bfloat16)
    low = (x - high.astype(jnp.float32)).astype(jnp.bfloat16)
    return jnp.concatenate([high, low], axis=0)


def patch_kernel(coords_ref, values_ref, phase_ref, out_ref):
    cells = lax.broadcasted_iota(jnp.int32, (PATCH, 1), 0).astype(jnp.float32)

    def one_block(i, carry):
        x = coords_ref[i, 0:1, :]
        y = coords_ref[i, 1:2, :]
        rows_kernel = jnp.exp2(((x - cells) ** 2) * gauss_scale)
        cols_kernel = jnp.exp2(((y - cells) ** 2) * gauss_scale)
        weighted = jnp.concatenate(
            [cols_kernel * values_ref[i, 0:1, :], cols_kernel * values_ref[i, 1:2, :]], axis=0
        )
        both = lax.dot_general(
            split_bf16(rows_kernel),
            split_bf16(weighted),
            (((1,), (1,)), ((), ())),
            preferred_element_type=jnp.float32,
        )
        width = 2 * PATCH
        plain = (both[:PATCH, :width] + both[:PATCH, width:]) + (
            both[PATCH:, :width] + both[PATCH:, width:]
        )
        real_part = plain[:, :PATCH]
        imag_part = plain[:, PATCH:]
        phase = phase_ref[pl.ds(i, 1), :]
        cos_b = phase[:, :PATCH]
        sin_b = phase[:, PATCH:]
        out_ref[i] = jnp.concatenate(
            [real_part * cos_b + imag_part * sin_b, imag_part * cos_b - real_part * sin_b],
            axis=1,
        )
        return carry

    lax.fori_loop(0, out_ref.shape[0], one_block, 0)


def make_phased_patches(vis_coords, vis_values, live, local):
    count = vis_coords.shape[0]
    step = 8
    phase = (jnp.arange(PATCH, dtype=jnp.int32)[None, :] * local[:, None]) % SG_PER
    angle = phase.astype(jnp.float32) * (2.0 * math.pi / SG_PER)
    keep = live.astype(jnp.float32)[:, None]
    phases = jnp.concatenate([jnp.cos(angle) * keep, jnp.sin(angle) * keep], axis=1)
    spec = pl.BlockSpec((step, 2, VIS), lambda i: (i, 0, 0))
    patch = pl.pallas_call(
        patch_kernel,
        grid=(count // step,),
        in_specs=[spec, spec, pl.BlockSpec((step, 2 * PATCH), lambda i: (i, 0))],
        out_specs=pl.BlockSpec((step, PATCH, 2 * PATCH), lambda i: (i, 0, 0)),
        out_shape=jax.ShapeDtypeStruct((count, PATCH, 2 * PATCH), jnp.float32),
        cost_estimate=pl.CostEstimate(
            flops=count * 4 * PATCH * 4 * PATCH * VIS * 2,
            transcendentals=count * 2 * PATCH * VIS,
            bytes_accessed=count * (4 * VIS + 2 * PATCH * PATCH) * 4,
        ),
    )(vis_coords, vis_values, phases)
    return patch.reshape(count, 2 * PATCH * PATCH)


def column_table():
    index = jnp.arange(SG, dtype=jnp.int32)
    phase = index[:, None] * index[None, :] % SG
    angle = phase.astype(jnp.float32) * (2.0 * math.pi / SG)
    scale = 1.0 / math.sqrt(SG)
    cosine = jnp.cos(angle) * scale
    sine = jnp.sin(angle) * scale
    return jnp.concatenate(
        [jnp.concatenate([cosine, -sine], 1), jnp.concatenate([sine, cosine], 1)], 0
    )


def body(
    vis_coords,
    vis_values,
    block_dest,
    block_local,
    block_tile,
    block_counts,
    facet_offsets,
    correction,
):
    n_tm = lax.axis_size("tm")
    n_sub = lax.axis_size("sub")
    devices = n_tm * n_sub
    blocks = vis_coords.shape[0]
    band_rows = SG // n_sub
    band_tiles = band_rows // PATCH
    col_tiles = SG // PATCH
    tiles_all = col_tiles * col_tiles
    chunk = SG // devices
    facet_rows = FS // n_sub

    live = jnp.arange(blocks, dtype=jnp.int32) < block_counts[0]
    patches = make_phased_patches(vis_coords, vis_values, live, block_local)

    target = block_dest[:, 0]
    row_tile = (target % n_sub) * band_tiles + block_tile // col_tiles
    tile_id = row_tile * col_tiles + block_tile % col_tiles
    placer = (
        tile_id[None, :] == jnp.arange(tiles_all, dtype=jnp.int32)[:, None]
    ).astype(jnp.float32)
    tiles = jnp.dot(placer, patches, precision=lax.Precision.HIGHEST)
    per_tile_row = PATCH // chunk
    outgoing = (
        tiles.reshape(col_tiles, col_tiles, per_tile_row, chunk, 2, PATCH)
        .transpose(0, 2, 3, 4, 1, 5)
        .reshape(devices, chunk, 2, SG)
    )
    arrived = lax.all_to_all(
        outgoing, ("tm", "sub"), split_axis=0, concat_axis=0, tiled=True
    )
    grid_rows = jnp.sum(arrived, axis=0).reshape(chunk, 2 * SG)
    spectrum = jnp.dot(grid_rows, column_table(), precision=lax.Precision.HIGHEST).reshape(
        chunk, 2, SG
    )

    offsets = jnp.clip(facet_offsets, 0, SG - FS)
    windows = jax.vmap(lambda start: lax.dynamic_slice_in_dim(spectrum, start, FS, 2))(
        offsets[:, 1]
    )
    windows = jnp.broadcast_to(
        windows[:, None], (n_tm, n_sub, chunk, 2, FS)
    ).reshape(devices, chunk, 2, FS)
    gathered = lax.all_to_all(
        windows, ("tm", "sub"), split_axis=0, concat_axis=0, tiled=True
    ).reshape(SG, 2, FS)

    facet = lax.axis_index("tm")
    band = lax.axis_index("sub")
    first_y = offsets[facet, 0] + band * facet_rows
    ys = first_y + jnp.arange(facet_rows, dtype=jnp.int32)
    rs = jnp.arange(SG, dtype=jnp.int32)
    angle = ((ys[:, None] * rs[None, :]) % SG).astype(jnp.float32) * (2.0 * math.pi / SG)
    scale = 1.0 / math.sqrt(SG)
    left = jnp.concatenate([jnp.cos(angle) * scale, jnp.sin(angle) * scale], 1)
    real_part = gathered[:, 0]
    imag_part = gathered[:, 1]
    right = jnp.concatenate(
        [
            jnp.concatenate([real_part, imag_part], 1),
            jnp.concatenate([imag_part, -real_part], 1),
        ],
        0,
    )
    summed = jnp.dot(left, right, precision=lax.Precision.HIGHEST).reshape(
        1, facet_rows, 2, FS
    )
    return summed * correction[:, :, None, :]


def solution(mesh):
    in_specs = (
        P(("tm", "sub"), None, None),
        P(("tm", "sub"), None, None),
        P(("tm", "sub"), None),
        P(("tm", "sub")),
        P(("tm", "sub")),
        P(("tm", "sub")),
        P(),
        P("tm", "sub", None),
    )
    out_specs = P("tm", "sub", None, None)
    return jax.shard_map(body, mesh=mesh, in_specs=in_specs, out_specs=out_specs, check_vma=False)
```

```python
import math

import jax
import jax.numpy as jnp
from jax import lax
from jax.experimental import pallas as pl
from jax.sharding import PartitionSpec as P

SG = 512
PATCH = 32
FS = 128
VIS = 1024
SG_PER = 16


kernel_width = 0.7
gauss_scale = -0.5 / (kernel_width * kernel_width) / math.log(2.0)


def split_bf16(x):
    high = x.astype(jnp.bfloat16)
    low = (x - high.astype(jnp.float32)).astype(jnp.bfloat16)
    return jnp.concatenate([high, low], axis=0)


def patch_kernel(coords_ref, values_ref, phase_ref, out_ref):
    cells = lax.broadcasted_iota(jnp.int32, (PATCH, 1), 0).astype(jnp.float32)

    def one_block(i, carry):
        x = coords_ref[i, 0:1, :]
        y = coords_ref[i, 1:2, :]
        rows_kernel = jnp.exp2(((x - cells) ** 2) * gauss_scale)
        cols_kernel = jnp.exp2(((y - cells) ** 2) * gauss_scale)
        weighted = jnp.concatenate(
            [cols_kernel * values_ref[i, 0:1, :], cols_kernel * values_ref[i, 1:2, :]], axis=0
        )
        both = lax.dot_general(
            split_bf16(rows_kernel),
            split_bf16(weighted),
            (((1,), (1,)), ((), ())),
            preferred_element_type=jnp.float32,
        )
        width = 2 * PATCH
        plain = (both[:PATCH, :width] + both[:PATCH, width:]) + (
            both[PATCH:, :width] + both[PATCH:, width:]
        )
        real_part = plain[:, :PATCH]
        imag_part = plain[:, PATCH:]
        phase = phase_ref[pl.ds(i, 1), :]
        cos_b = phase[:, :PATCH]
        sin_b = phase[:, PATCH:]
        out_ref[i] = jnp.concatenate(
            [real_part * cos_b + imag_part * sin_b, imag_part * cos_b - real_part * sin_b],
            axis=1,
        )
        return carry

    lax.fori_loop(0, out_ref.shape[0], one_block, 0)


def make_phased_patches(vis_coords, vis_values, live, local):
    count = vis_coords.shape[0]
    step = 8
    phase = (jnp.arange(PATCH, dtype=jnp.int32)[None, :] * local[:, None]) % SG_PER
    angle = phase.astype(jnp.float32) * (2.0 * math.pi / SG_PER)
    keep = live.astype(jnp.float32)[:, None]
    phases = jnp.concatenate([jnp.cos(angle) * keep, jnp.sin(angle) * keep], axis=1)
    spec = pl.BlockSpec((step, 2, VIS), lambda i: (i, 0, 0))
    patch = pl.pallas_call(
        patch_kernel,
        grid=(count // step,),
        in_specs=[spec, spec, pl.BlockSpec((step, 2 * PATCH), lambda i: (i, 0))],
        out_specs=pl.BlockSpec((step, PATCH, 2 * PATCH), lambda i: (i, 0, 0)),
        out_shape=jax.ShapeDtypeStruct((count, PATCH, 2 * PATCH), jnp.float32),
        cost_estimate=pl.CostEstimate(
            flops=count * 4 * PATCH * 4 * PATCH * VIS * 2,
            transcendentals=count * 2 * PATCH * VIS,
            bytes_accessed=count * (4 * VIS + 2 * PATCH * PATCH) * 4,
        ),
    )(vis_coords, vis_values, phases)
    return patch.reshape(count, 2 * PATCH * PATCH)


def column_table():
    index = jnp.arange(SG, dtype=jnp.int32)
    phase = index[:, None] * index[None, :] % SG
    angle = phase.astype(jnp.float32) * (2.0 * math.pi / SG)
    scale = 1.0 / math.sqrt(SG)
    cosine = jnp.cos(angle) * scale
    sine = jnp.sin(angle) * scale
    return jnp.concatenate(
        [jnp.concatenate([cosine, -sine], 1), jnp.concatenate([sine, cosine], 1)], 0
    )


def body(
    vis_coords,
    vis_values,
    block_dest,
    block_local,
    block_tile,
    block_counts,
    facet_offsets,
    correction,
):
    n_tm = lax.axis_size("tm")
    n_sub = lax.axis_size("sub")
    devices = n_tm * n_sub
    blocks = vis_coords.shape[0]
    band_rows = SG // n_sub
    band_tiles = band_rows // PATCH
    col_tiles = SG // PATCH
    tiles_all = col_tiles * col_tiles
    chunk = SG // devices
    facet_rows = FS // n_sub

    live = jnp.arange(blocks, dtype=jnp.int32) < block_counts[0]
    patches = make_phased_patches(vis_coords, vis_values, live, block_local)

    target = block_dest[:, 0]
    row_tile = (target % n_sub) * band_tiles + block_tile // col_tiles
    tile_id = row_tile * col_tiles + block_tile % col_tiles
    placer = (
        tile_id[None, :] == jnp.arange(tiles_all, dtype=jnp.int32)[:, None]
    ).astype(jnp.float32)
    tiles = jnp.dot(placer, patches, precision=lax.Precision.HIGHEST)
    grid = (
        tiles.reshape(col_tiles, col_tiles, PATCH, 2, PATCH)
        .transpose(0, 2, 3, 1, 4)
        .reshape(2, SG // 2, 2, SG)
    )
    core = lax.axis_index("tm") % 2
    keep = jnp.where(core == 0, grid[0], grid[1])
    give = jnp.where(core == 0, grid[1], grid[0])
    pair = [(i, i ^ 1) for i in range(n_tm)]
    chip_half = keep + lax.ppermute(give, "tm", pair)
    half_chunk = chunk // 2
    arrived = lax.all_to_all(
        chip_half.reshape(devices, half_chunk, 2, SG),
        ("tm", "sub"),
        split_axis=0,
        concat_axis=0,
        tiled=True,
    )
    grid_rows = jnp.sum(
        arrived.reshape(n_tm // 2, 2, n_sub, half_chunk, 2, SG), axis=(0, 2)
    ).reshape(chunk, 2 * SG)
    spectrum = jnp.dot(grid_rows, column_table(), precision=lax.Precision.HIGHEST).reshape(
        chunk, 2, SG
    )

    offsets = jnp.clip(facet_offsets, 0, SG - FS)
    windows = jax.vmap(lambda start: lax.dynamic_slice_in_dim(spectrum, start, FS, 2))(
        offsets[:, 1]
    )
    windows = jnp.broadcast_to(
        windows[:, None], (n_tm, n_sub, chunk, 2, FS)
    ).reshape(devices, chunk, 2, FS)
    gathered = lax.all_to_all(
        windows, ("tm", "sub"), split_axis=0, concat_axis=0, tiled=True
    ).reshape(SG, 2, FS)

    facet = lax.axis_index("tm")
    band = lax.axis_index("sub")
    first_y = offsets[facet, 0] + band * facet_rows
    ys = first_y + jnp.arange(facet_rows, dtype=jnp.int32)
    order = jnp.arange(SG, dtype=jnp.int32)
    rs = (
        ((order // half_chunk) % 2) * (SG // 2)
        + (order // chunk) * half_chunk
        + order % half_chunk
    )
    angle = ((ys[:, None] * rs[None, :]) % SG).astype(jnp.float32) * (2.0 * math.pi / SG)
    scale = 1.0 / math.sqrt(SG)
    left = jnp.concatenate([jnp.cos(angle) * scale, jnp.sin(angle) * scale], 1)
    real_part = gathered[:, 0]
    imag_part = gathered[:, 1]
    right = jnp.concatenate(
        [
            jnp.concatenate([real_part, imag_part], 1),
            jnp.concatenate([imag_part, -real_part], 1),
        ],
        0,
    )
    summed = jnp.dot(left, right, precision=lax.Precision.HIGHEST).reshape(
        1, facet_rows, 2, FS
    )
    return summed * correction[:, :, None, :]


def solution(mesh):
    in_specs = (
        P(("tm", "sub"), None, None),
        P(("tm", "sub"), None, None),
        P(("tm", "sub"), None),
        P(("tm", "sub")),
        P(("tm", "sub")),
        P(("tm", "sub")),
        P(),
        P("tm", "sub", None),
    )
    out_specs = P("tm", "sub", None, None)
    return jax.shard_map(body, mesh=mesh, in_specs=in_specs, out_specs=out_specs, check_vma=False)
```

```python
import math

import jax
import jax.numpy as jnp
from jax import lax
from jax.experimental import pallas as pl
from jax.sharding import PartitionSpec as P

SG = 512
PATCH = 32
FS = 128
VIS = 1024
SG_PER = 16


kernel_width = 0.7
gauss_scale = -0.5 / (kernel_width * kernel_width) / math.log(2.0)


def split_bf16(x):
    high = x.astype(jnp.bfloat16)
    low = (x - high.astype(jnp.float32)).astype(jnp.bfloat16)
    return jnp.concatenate([high, low], axis=0)


def patch_kernel(coords_ref, values_ref, phase_ref, out_ref):
    cells = lax.broadcasted_iota(jnp.int32, (PATCH, 1), 0).astype(jnp.float32)

    def one_block(i, carry):
        x = coords_ref[i, 0:1, :]
        y = coords_ref[i, 1:2, :]
        rows_kernel = jnp.exp2(((x - cells) ** 2) * gauss_scale)
        cols_kernel = jnp.exp2(((y - cells) ** 2) * gauss_scale)
        weighted = jnp.concatenate(
            [cols_kernel * values_ref[i, 0:1, :], cols_kernel * values_ref[i, 1:2, :]], axis=0
        )
        both = lax.dot_general(
            split_bf16(rows_kernel),
            split_bf16(weighted),
            (((1,), (1,)), ((), ())),
            preferred_element_type=jnp.float32,
        )
        width = 2 * PATCH
        plain = (both[:PATCH, :width] + both[:PATCH, width:]) + (
            both[PATCH:, :width] + both[PATCH:, width:]
        )
        real_part = plain[:, :PATCH]
        imag_part = plain[:, PATCH:]
        phase = phase_ref[pl.ds(i, 1), :]
        cos_b = phase[:, :PATCH]
        sin_b = phase[:, PATCH:]
        out_ref[i] = jnp.concatenate(
            [real_part * cos_b + imag_part * sin_b, imag_part * cos_b - real_part * sin_b],
            axis=1,
        )
        return carry

    lax.fori_loop(0, out_ref.shape[0], one_block, 0)


def make_phased_patches(vis_coords, vis_values, live, local):
    count = vis_coords.shape[0]
    step = 8
    phase = (jnp.arange(PATCH, dtype=jnp.int32)[None, :] * local[:, None]) % SG_PER
    angle = phase.astype(jnp.float32) * (2.0 * math.pi / SG_PER)
    keep = live.astype(jnp.float32)[:, None]
    phases = jnp.concatenate([jnp.cos(angle) * keep, jnp.sin(angle) * keep], axis=1)
    spec = pl.BlockSpec((step, 2, VIS), lambda i: (i, 0, 0))
    patch = pl.pallas_call(
        patch_kernel,
        grid=(count // step,),
        in_specs=[spec, spec, pl.BlockSpec((step, 2 * PATCH), lambda i: (i, 0))],
        out_specs=pl.BlockSpec((step, PATCH, 2 * PATCH), lambda i: (i, 0, 0)),
        out_shape=jax.ShapeDtypeStruct((count, PATCH, 2 * PATCH), jnp.float32),
        cost_estimate=pl.CostEstimate(
            flops=count * 4 * PATCH * 4 * PATCH * VIS * 2,
            transcendentals=count * 2 * PATCH * VIS,
            bytes_accessed=count * (4 * VIS + 2 * PATCH * PATCH) * 4,
        ),
    )(vis_coords, vis_values, phases)
    return patch.reshape(count, 2 * PATCH * PATCH)


def column_table():
    index = jnp.arange(SG, dtype=jnp.int32)
    phase = index[:, None] * index[None, :] % SG
    angle = phase.astype(jnp.float32) * (2.0 * math.pi / SG)
    scale = 1.0 / math.sqrt(SG)
    cosine = jnp.cos(angle) * scale
    sine = jnp.sin(angle) * scale
    return jnp.concatenate(
        [jnp.concatenate([cosine, -sine], 1), jnp.concatenate([sine, cosine], 1)], 0
    )


def body(
    vis_coords,
    vis_values,
    block_dest,
    block_local,
    block_tile,
    block_counts,
    facet_offsets,
    correction,
):
    n_tm = lax.axis_size("tm")
    n_sub = lax.axis_size("sub")
    devices = n_tm * n_sub
    blocks = vis_coords.shape[0]
    band_rows = SG // n_sub
    band_tiles = band_rows // PATCH
    col_tiles = SG // PATCH
    tiles_all = col_tiles * col_tiles
    chunk = SG // devices
    facet_rows = FS // n_sub

    live = jnp.arange(blocks, dtype=jnp.int32) < block_counts[0]
    patches = make_phased_patches(vis_coords, vis_values, live, block_local)

    target = block_dest[:, 0]
    row_tile = (target % n_sub) * band_tiles + block_tile // col_tiles
    core = lax.axis_index("tm") % 2
    row_tile = (row_tile + core * (col_tiles // 2)) % col_tiles
    tile_id = row_tile * col_tiles + block_tile % col_tiles
    placer = (
        tile_id[None, :] == jnp.arange(tiles_all, dtype=jnp.int32)[:, None]
    ).astype(jnp.float32)
    tiles = jnp.dot(placer, patches, precision=lax.Precision.HIGHEST)
    grid = (
        tiles.reshape(col_tiles, col_tiles, PATCH, 2, PATCH)
        .transpose(0, 2, 3, 1, 4)
        .reshape(2, SG // 2, 2, SG)
    )
    pair = [(i, i ^ 1) for i in range(n_tm)]
    chip_half = grid[0] + lax.ppermute(grid[1], "tm", pair)
    half_chunk = chunk // 2
    arrived = lax.all_to_all(
        chip_half.reshape(devices, half_chunk, 2, SG),
        ("tm", "sub"),
        split_axis=0,
        concat_axis=0,
        tiled=True,
    )
    grid_rows = jnp.sum(
        arrived.reshape(n_tm // 2, 2, n_sub, half_chunk, 2, SG), axis=(0, 2)
    ).reshape(chunk, 2 * SG)
    spectrum = jnp.dot(grid_rows, column_table(), precision=lax.Precision.HIGHEST).reshape(
        chunk, 2, SG
    )

    offsets = jnp.clip(facet_offsets, 0, SG - FS)
    windows = jnp.stack(
        [lax.dynamic_slice_in_dim(spectrum, offsets[f, 1], FS, 2) for f in range(n_tm)]
    )
    windows = jnp.broadcast_to(
        windows[:, None], (n_tm, n_sub, chunk, 2, FS)
    ).reshape(devices, chunk, 2, FS)
    gathered = lax.all_to_all(
        windows, ("tm", "sub"), split_axis=0, concat_axis=0, tiled=True
    ).reshape(SG, 2, FS)

    facet = lax.axis_index("tm")
    band = lax.axis_index("sub")
    first_y = offsets[facet, 0] + band * facet_rows
    ys = first_y + jnp.arange(facet_rows, dtype=jnp.int32)
    order = jnp.arange(SG, dtype=jnp.int32)
    rs = (
        ((order // half_chunk) % 2) * (SG // 2)
        + (order // chunk) * half_chunk
        + order % half_chunk
    )
    angle = ((ys[:, None] * rs[None, :]) % SG).astype(jnp.float32) * (2.0 * math.pi / SG)
    scale = 1.0 / math.sqrt(SG)
    left = jnp.concatenate([jnp.cos(angle) * scale, jnp.sin(angle) * scale], 1)
    real_part = gathered[:, 0]
    imag_part = gathered[:, 1]
    right = jnp.concatenate(
        [
            jnp.concatenate([real_part, imag_part], 1),
            jnp.concatenate([imag_part, -real_part], 1),
        ],
        0,
    )
    summed = jnp.dot(left, right, precision=lax.Precision.HIGHEST).reshape(
        1, facet_rows, 2, FS
    )
    return summed * correction[:, :, None, :]


def solution(mesh):
    in_specs = (
        P(("tm", "sub"), None, None),
        P(("tm", "sub"), None, None),
        P(("tm", "sub"), None),
        P(("tm", "sub")),
        P(("tm", "sub")),
        P(("tm", "sub")),
        P(),
        P("tm", "sub", None),
    )
    out_specs = P("tm", "sub", None, None)
    return jax.shard_map(body, mesh=mesh, in_specs=in_specs, out_specs=out_specs, check_vma=False)
```

```python
import math

import jax
import jax.numpy as jnp
from jax import lax
from jax.experimental import pallas as pl
from jax.sharding import PartitionSpec as P

SG = 512
PATCH = 32
FS = 128
VIS = 1024
SG_PER = 16


kernel_width = 0.7
gauss_scale = -0.5 / (kernel_width * kernel_width) / math.log(2.0)


def split_bf16(x):
    high = x.astype(jnp.bfloat16)
    low = (x - high.astype(jnp.float32)).astype(jnp.bfloat16)
    return jnp.concatenate([high, low], axis=0)


def patch_kernel(coords_ref, values_ref, phase_ref, out_ref):
    cells = lax.broadcasted_iota(jnp.int32, (PATCH, 1), 0).astype(jnp.float32)

    def one_block(i, carry):
        x = coords_ref[i, 0:1, :]
        y = coords_ref[i, 1:2, :]
        rows_kernel = jnp.exp2(((x - cells) ** 2) * gauss_scale)
        cols_kernel = jnp.exp2(((y - cells) ** 2) * gauss_scale)
        weighted = jnp.concatenate(
            [cols_kernel * values_ref[i, 0:1, :], cols_kernel * values_ref[i, 1:2, :]], axis=0
        )
        both = lax.dot_general(
            split_bf16(rows_kernel),
            split_bf16(weighted),
            (((1,), (1,)), ((), ())),
            preferred_element_type=jnp.float32,
        )
        width = 2 * PATCH
        plain = (both[:PATCH, :width] + both[:PATCH, width:]) + (
            both[PATCH:, :width] + both[PATCH:, width:]
        )
        real_part = plain[:, :PATCH]
        imag_part = plain[:, PATCH:]
        phase = phase_ref[pl.ds(i, 1), :]
        cos_b = phase[:, :PATCH]
        sin_b = phase[:, PATCH:]
        out_ref[i] = jnp.concatenate(
            [real_part * cos_b + imag_part * sin_b, imag_part * cos_b - real_part * sin_b],
            axis=1,
        )
        return carry

    lax.fori_loop(0, out_ref.shape[0], one_block, 0)


def make_phased_patches(vis_coords, vis_values, live, local):
    count = vis_coords.shape[0]
    step = 8
    phase = (jnp.arange(PATCH, dtype=jnp.int32)[None, :] * local[:, None]) % SG_PER
    angle = phase.astype(jnp.float32) * (2.0 * math.pi / SG_PER)
    keep = live.astype(jnp.float32)[:, None]
    phases = jnp.concatenate([jnp.cos(angle) * keep, jnp.sin(angle) * keep], axis=1)
    spec = pl.BlockSpec((step, 2, VIS), lambda i: (i, 0, 0))
    patch = pl.pallas_call(
        patch_kernel,
        grid=(count // step,),
        in_specs=[spec, spec, pl.BlockSpec((step, 2 * PATCH), lambda i: (i, 0))],
        out_specs=pl.BlockSpec((step, PATCH, 2 * PATCH), lambda i: (i, 0, 0)),
        out_shape=jax.ShapeDtypeStruct((count, PATCH, 2 * PATCH), jnp.float32),
        cost_estimate=pl.CostEstimate(
            flops=count * 4 * PATCH * 4 * PATCH * VIS * 2,
            transcendentals=count * 2 * PATCH * VIS,
            bytes_accessed=count * (4 * VIS + 2 * PATCH * PATCH) * 4,
        ),
    )(vis_coords, vis_values, phases)
    return patch.reshape(count, 2 * PATCH * PATCH)


def window_table():
    cs = jnp.arange(SG, dtype=jnp.int32)
    xs = jnp.arange(FS, dtype=jnp.int32)
    angle = ((cs[:, None] * xs[None, :]) % SG).astype(jnp.float32) * (2.0 * math.pi / SG)
    scale = 1.0 / math.sqrt(SG)
    cosine = jnp.cos(angle) * scale
    sine = jnp.sin(angle) * scale
    return jnp.concatenate(
        [jnp.concatenate([cosine, -sine], 1), jnp.concatenate([sine, cosine], 1)], 0
    )


def body(
    vis_coords,
    vis_values,
    block_dest,
    block_local,
    block_tile,
    block_counts,
    facet_offsets,
    correction,
):
    n_tm = lax.axis_size("tm")
    n_sub = lax.axis_size("sub")
    devices = n_tm * n_sub
    blocks = vis_coords.shape[0]
    band_rows = SG // n_sub
    band_tiles = band_rows // PATCH
    col_tiles = SG // PATCH
    tiles_all = col_tiles * col_tiles
    chunk = SG // devices
    facet_rows = FS // n_sub

    live = jnp.arange(blocks, dtype=jnp.int32) < block_counts[0]
    patches = make_phased_patches(vis_coords, vis_values, live, block_local)

    target = block_dest[:, 0]
    row_tile = (target % n_sub) * band_tiles + block_tile // col_tiles
    core = lax.axis_index("tm") % 2
    row_tile = (row_tile + core * (col_tiles // 2)) % col_tiles
    tile_id = row_tile * col_tiles + block_tile % col_tiles
    placer = (
        tile_id[None, :] == jnp.arange(tiles_all, dtype=jnp.int32)[:, None]
    ).astype(jnp.float32)
    tiles = jnp.dot(placer, patches, precision=lax.Precision.HIGHEST)
    half_tiles = tiles_all // 2

    def to_rows(part):
        return (
            part.reshape(col_tiles // 2, col_tiles, PATCH, 2, PATCH)
            .transpose(0, 2, 3, 1, 4)
            .reshape(SG // 2, 2, SG)
        )

    pair = [(i, i ^ 1) for i in range(n_tm)]
    chip_half = to_rows(tiles[:half_tiles]) + lax.ppermute(
        to_rows(tiles[half_tiles:]), "tm", pair
    )
    half_chunk = chunk // 2
    arrived = lax.all_to_all(
        chip_half.reshape(devices, half_chunk, 2, SG),
        ("tm", "sub"),
        split_axis=0,
        concat_axis=0,
        tiled=True,
    )
    grid_rows = jnp.sum(
        arrived.reshape(n_tm // 2, 2, n_sub, half_chunk, 2, SG), axis=(0, 2)
    ).reshape(chunk, 2 * SG)
    offsets = jnp.clip(facet_offsets, 0, SG - FS)
    cs = jnp.arange(SG, dtype=jnp.int32)
    shift = ((offsets[:, 1][:, None] * cs[None, :]) % SG).astype(jnp.float32) * (
        2.0 * math.pi / SG
    )
    cos_s = jnp.cos(shift)[:, None, :]
    sin_s = jnp.sin(shift)[:, None, :]
    g_re = grid_rows[None, :, :SG]
    g_im = grid_rows[None, :, SG:]
    shifted = jnp.concatenate(
        [g_re * cos_s + g_im * sin_s, g_im * cos_s - g_re * sin_s], axis=2
    ).reshape(n_tm * chunk, 2 * SG)
    windows = jnp.dot(shifted, window_table(), precision=lax.Precision.HIGHEST).reshape(
        n_tm, chunk, 2, FS
    )
    windows = jnp.broadcast_to(
        windows[:, None], (n_tm, n_sub, chunk, 2, FS)
    ).reshape(devices, chunk, 2, FS)
    gathered = lax.all_to_all(
        windows, ("tm", "sub"), split_axis=0, concat_axis=0, tiled=True
    ).reshape(SG, 2, FS)

    facet = lax.axis_index("tm")
    band = lax.axis_index("sub")
    first_y = offsets[facet, 0] + band * facet_rows
    ys = first_y + jnp.arange(facet_rows, dtype=jnp.int32)
    order = jnp.arange(SG, dtype=jnp.int32)
    rs = (
        ((order // half_chunk) % 2) * (SG // 2)
        + (order // chunk) * half_chunk
        + order % half_chunk
    )
    angle = ((ys[:, None] * rs[None, :]) % SG).astype(jnp.float32) * (2.0 * math.pi / SG)
    scale = 1.0 / math.sqrt(SG)
    left = jnp.concatenate([jnp.cos(angle) * scale, jnp.sin(angle) * scale], 1)
    real_part = gathered[:, 0]
    imag_part = gathered[:, 1]
    right = jnp.concatenate(
        [
            jnp.concatenate([real_part, imag_part], 1),
            jnp.concatenate([imag_part, -real_part], 1),
        ],
        0,
    )
    summed = jnp.dot(left, right, precision=lax.Precision.HIGHEST).reshape(
        1, facet_rows, 2, FS
    )
    return summed * correction[:, :, None, :]


def solution(mesh):
    in_specs = (
        P(("tm", "sub"), None, None),
        P(("tm", "sub"), None, None),
        P(("tm", "sub"), None),
        P(("tm", "sub")),
        P(("tm", "sub")),
        P(("tm", "sub")),
        P(),
        P("tm", "sub", None),
    )
    out_specs = P("tm", "sub", None, None)
    return jax.shard_map(body, mesh=mesh, in_specs=in_specs, out_specs=out_specs, check_vma=False)
```

```python
import math

import jax
import jax.numpy as jnp
from jax import lax
from jax.experimental import pallas as pl
from jax.experimental.pallas import tpu as pltpu
from jax.sharding import PartitionSpec as P

SG = 512
PATCH = 32
FS = 128
VIS = 1024
SG_PER = 16


kernel_width = 0.7
gauss_scale = -0.5 / (kernel_width * kernel_width) / math.log(2.0)


def split_bf16(x):
    high = x.astype(jnp.bfloat16)
    low = (x - high.astype(jnp.float32)).astype(jnp.bfloat16)
    return jnp.concatenate([high, low], axis=0)


def patch_kernel(place_ref, coords_ref, values_ref, phase_ref, out_ref):
    step = coords_ref.shape[0]
    cells = lax.broadcasted_iota(jnp.int32, (PATCH, 1), 0).astype(jnp.float32)
    slot = lax.broadcasted_iota(jnp.int32, (PATCH, 128), 1) // PATCH
    half = out_ref.shape[1] // 2
    per_group = 128 // PATCH

    @pl.when(pl.program_id(0) == 0)
    def _():
        out_ref[...] = jnp.zeros_like(out_ref)

    def one_block(i, carry):
        x = coords_ref[i, 0:1, :]
        y = coords_ref[i, 1:2, :]
        rows_kernel = jnp.exp2(((x - cells) ** 2) * gauss_scale)
        cols_kernel = jnp.exp2(((y - cells) ** 2) * gauss_scale)
        weighted = jnp.concatenate(
            [cols_kernel * values_ref[i, 0:1, :], cols_kernel * values_ref[i, 1:2, :]], axis=0
        )
        both = lax.dot_general(
            split_bf16(rows_kernel),
            split_bf16(weighted),
            (((1,), (1,)), ((), ())),
            preferred_element_type=jnp.float32,
        )
        width = 2 * PATCH
        plain = (both[:PATCH, :width] + both[:PATCH, width:]) + (
            both[PATCH:, :width] + both[PATCH:, width:]
        )
        real_part = plain[:, :PATCH]
        imag_part = plain[:, PATCH:]
        phase = phase_ref[pl.ds(i, 1), :]
        cos_b = phase[:, :PATCH]
        sin_b = phase[:, PATCH:]
        phased = (
            real_part * cos_b + imag_part * sin_b,
            imag_part * cos_b - real_part * sin_b,
        )
        tile = place_ref[pl.program_id(0) * step + i]
        row_tile = tile // (SG // PATCH)
        col_tile = tile % (SG // PATCH)
        rows = pl.ds(pl.multiple_of(row_tile * PATCH, PATCH), PATCH)
        keep = slot == col_tile % per_group
        for part, values in enumerate(phased):
            start = pl.multiple_of(part * half + (col_tile // per_group) * 128, 128)
            spread = jnp.concatenate([values] * per_group, axis=1)
            out_ref[rows, pl.ds(start, 128)] += jnp.where(keep, spread, 0.0)
        return carry

    lax.fori_loop(0, step, one_block, 0)


def make_phased_grid(vis_coords, vis_values, live, local, tile_id):
    count = vis_coords.shape[0]
    step = 8
    phase = (jnp.arange(PATCH, dtype=jnp.int32)[None, :] * local[:, None]) % SG_PER
    angle = phase.astype(jnp.float32) * (2.0 * math.pi / SG_PER)
    keep = live.astype(jnp.float32)[:, None]
    phases = jnp.concatenate([jnp.cos(angle) * keep, jnp.sin(angle) * keep], axis=1)
    spec = pl.BlockSpec((step, 2, VIS), lambda i, place: (i, 0, 0))
    return pl.pallas_call(
        patch_kernel,
        grid_spec=pltpu.PrefetchScalarGridSpec(
            num_scalar_prefetch=1,
            grid=(count // step,),
            in_specs=[
                spec,
                spec,
                pl.BlockSpec((step, 2 * PATCH), lambda i, place: (i, 0)),
            ],
            out_specs=pl.BlockSpec((SG, 2 * SG), lambda i, place: (0, 0)),
        ),
        out_shape=jax.ShapeDtypeStruct((SG, 2 * SG), jnp.float32),
        cost_estimate=pl.CostEstimate(
            flops=count * 4 * PATCH * 4 * PATCH * VIS * 2,
            transcendentals=count * 2 * PATCH * VIS,
            bytes_accessed=count * 4 * VIS * 4 + SG * SG * 8,
        ),
    )(tile_id, vis_coords, vis_values, phases)


def window_table():
    cs = jnp.arange(SG, dtype=jnp.int32)
    xs = jnp.arange(FS, dtype=jnp.int32)
    angle = ((cs[:, None] * xs[None, :]) % SG).astype(jnp.float32) * (2.0 * math.pi / SG)
    scale = 1.0 / math.sqrt(SG)
    cosine = jnp.cos(angle) * scale
    sine = jnp.sin(angle) * scale
    return jnp.concatenate(
        [jnp.concatenate([cosine, -sine], 1), jnp.concatenate([sine, cosine], 1)], 0
    )


def body(
    vis_coords,
    vis_values,
    block_dest,
    block_local,
    block_tile,
    block_counts,
    facet_offsets,
    correction,
):
    n_tm = lax.axis_size("tm")
    n_sub = lax.axis_size("sub")
    devices = n_tm * n_sub
    blocks = vis_coords.shape[0]
    band_rows = SG // n_sub
    band_tiles = band_rows // PATCH
    col_tiles = SG // PATCH
    tiles_all = col_tiles * col_tiles
    chunk = SG // devices
    facet_rows = FS // n_sub

    live = jnp.arange(blocks, dtype=jnp.int32) < block_counts[0]
    target = block_dest[:, 0]
    row_tile = (target % n_sub) * band_tiles + block_tile // col_tiles
    core = lax.axis_index("tm") % 2
    row_tile = (row_tile + core * (col_tiles // 2)) % col_tiles
    tile_id = row_tile * col_tiles + block_tile % col_tiles
    grid = make_phased_grid(vis_coords, vis_values, live, block_local, tile_id)

    pair = [(i, i ^ 1) for i in range(n_tm)]
    chip_half = grid[: SG // 2] + lax.ppermute(grid[SG // 2 :], "tm", pair)
    half_chunk = chunk // 2
    arrived = lax.all_to_all(
        chip_half.reshape(devices, half_chunk, 2, SG),
        ("tm", "sub"),
        split_axis=0,
        concat_axis=0,
        tiled=True,
    )
    grid_rows = jnp.sum(
        arrived.reshape(n_tm // 2, 2, n_sub, half_chunk, 2, SG), axis=(0, 2)
    ).reshape(chunk, 2 * SG)
    offsets = jnp.clip(facet_offsets, 0, SG - FS)
    cs = jnp.arange(SG, dtype=jnp.int32)
    shift = ((offsets[:, 1][:, None] * cs[None, :]) % SG).astype(jnp.float32) * (
        2.0 * math.pi / SG
    )
    cos_s = jnp.cos(shift)[:, None, :]
    sin_s = jnp.sin(shift)[:, None, :]
    g_re = grid_rows[None, :, :SG]
    g_im = grid_rows[None, :, SG:]
    shifted = jnp.concatenate(
        [g_re * cos_s + g_im * sin_s, g_im * cos_s - g_re * sin_s], axis=2
    ).reshape(n_tm * chunk, 2 * SG)
    windows = jnp.dot(shifted, window_table(), precision=lax.Precision.HIGHEST).reshape(
        n_tm, chunk, 2, FS
    )
    windows = jnp.broadcast_to(
        windows[:, None], (n_tm, n_sub, chunk, 2, FS)
    ).reshape(devices, chunk, 2, FS)
    gathered = lax.all_to_all(
        windows, ("tm", "sub"), split_axis=0, concat_axis=0, tiled=True
    ).reshape(SG, 2, FS)

    facet = lax.axis_index("tm")
    band = lax.axis_index("sub")
    first_y = offsets[facet, 0] + band * facet_rows
    ys = first_y + jnp.arange(facet_rows, dtype=jnp.int32)
    order = jnp.arange(SG, dtype=jnp.int32)
    rs = (
        ((order // half_chunk) % 2) * (SG // 2)
        + (order // chunk) * half_chunk
        + order % half_chunk
    )
    angle = ((ys[:, None] * rs[None, :]) % SG).astype(jnp.float32) * (2.0 * math.pi / SG)
    scale = 1.0 / math.sqrt(SG)
    left = jnp.concatenate([jnp.cos(angle) * scale, jnp.sin(angle) * scale], 1)
    real_part = gathered[:, 0]
    imag_part = gathered[:, 1]
    right = jnp.concatenate(
        [
            jnp.concatenate([real_part, imag_part], 1),
            jnp.concatenate([imag_part, -real_part], 1),
        ],
        0,
    )
    summed = jnp.dot(left, right, precision=lax.Precision.HIGHEST).reshape(
        1, facet_rows, 2, FS
    )
    return summed * correction[:, :, None, :]


def solution(mesh):
    in_specs = (
        P(("tm", "sub"), None, None),
        P(("tm", "sub"), None, None),
        P(("tm", "sub"), None),
        P(("tm", "sub")),
        P(("tm", "sub")),
        P(("tm", "sub")),
        P(),
        P("tm", "sub", None),
    )
    out_specs = P("tm", "sub", None, None)
    return jax.shard_map(body, mesh=mesh, in_specs=in_specs, out_specs=out_specs, check_vma=False)
```

```python
import math

import jax
import jax.numpy as jnp
from jax import lax
from jax.experimental import pallas as pl
from jax.experimental.pallas import tpu as pltpu
from jax.sharding import PartitionSpec as P

SG = 512
PATCH = 32
FS = 128
VIS = 1024
VIS_PART = 512
SG_PER = 16


kernel_width = 0.7
gauss_scale = -0.5 / (kernel_width * kernel_width) / math.log(2.0)


def split_bf16(x):
    high = x.astype(jnp.bfloat16)
    low = (x - high.astype(jnp.float32)).astype(jnp.bfloat16)
    return jnp.concatenate([high, low], axis=0)


def patch_kernel(place_ref, coords_ref, values_ref, phase_ref, out_ref):
    step = coords_ref.shape[0]
    cells = lax.broadcasted_iota(jnp.int32, (PATCH, 1), 0).astype(jnp.float32)
    pad = jnp.zeros((PATCH, 128 - PATCH), jnp.float32)
    half = out_ref.shape[1] // 2
    per_group = 128 // PATCH

    @pl.when(pl.program_id(0) == 0)
    def _():
        out_ref[...] = jnp.zeros_like(out_ref)

    def one_block(i, carry):
        both = None
        for part in range(VIS // VIS_PART):
            lanes = pl.ds(part * VIS_PART, VIS_PART)
            x = coords_ref[i, 0:1, lanes]
            y = coords_ref[i, 1:2, lanes]
            rows_kernel = jnp.exp2(((x - cells) ** 2) * gauss_scale)
            cols_kernel = jnp.exp2(((y - cells) ** 2) * gauss_scale)
            weighted = jnp.concatenate(
                [cols_kernel * values_ref[i, 0:1, lanes], cols_kernel * values_ref[i, 1:2, lanes]],
                axis=0,
            )
            term = lax.dot_general(
                split_bf16(rows_kernel),
                split_bf16(weighted),
                (((1,), (1,)), ((), ())),
                preferred_element_type=jnp.float32,
            )
            both = term if both is None else both + term
        width = 2 * PATCH
        plain = (both[:PATCH, :width] + both[:PATCH, width:]) + (
            both[PATCH:, :width] + both[PATCH:, width:]
        )
        real_part = plain[:, :PATCH]
        imag_part = plain[:, PATCH:]
        phase = phase_ref[pl.ds(i, 1), :]
        cos_b = phase[:, :PATCH]
        sin_b = phase[:, PATCH:]
        phased = (
            real_part * cos_b + imag_part * sin_b,
            imag_part * cos_b - real_part * sin_b,
        )
        tile = place_ref[pl.program_id(0) * step + i]
        row_tile = tile // (SG // PATCH)
        col_tile = tile % (SG // PATCH)
        rows = pl.ds(pl.multiple_of(row_tile * PATCH, PATCH), PATCH)
        shift = (col_tile % per_group) * PATCH
        for part, values in enumerate(phased):
            start = pl.multiple_of(part * half + (col_tile // per_group) * 128, 128)
            padded = jnp.concatenate([values, pad], axis=1)
            out_ref[rows, pl.ds(start, 128)] += pltpu.roll(padded, shift, 1)
        return carry

    lax.fori_loop(0, step, one_block, 0)


def make_phased_grid(vis_coords, vis_values, live, local, tile_id):
    count = vis_coords.shape[0]
    step = 8
    phase = (jnp.arange(PATCH, dtype=jnp.int32)[None, :] * local[:, None]) % SG_PER
    angle = phase.astype(jnp.float32) * (2.0 * math.pi / SG_PER)
    keep = live.astype(jnp.float32)[:, None]
    phases = jnp.concatenate([jnp.cos(angle) * keep, jnp.sin(angle) * keep], axis=1)
    spec = pl.BlockSpec((step, 2, VIS), lambda i, place: (i, 0, 0))
    return pl.pallas_call(
        patch_kernel,
        grid_spec=pltpu.PrefetchScalarGridSpec(
            num_scalar_prefetch=1,
            grid=(count // step,),
            in_specs=[
                spec,
                spec,
                pl.BlockSpec((step, 2 * PATCH), lambda i, place: (i, 0)),
            ],
            out_specs=pl.BlockSpec((SG, 2 * SG), lambda i, place: (0, 0)),
        ),
        out_shape=jax.ShapeDtypeStruct((SG, 2 * SG), jnp.float32),
        cost_estimate=pl.CostEstimate(
            flops=count * 4 * PATCH * 4 * PATCH * VIS * 2,
            transcendentals=count * 2 * PATCH * VIS,
            bytes_accessed=count * 4 * VIS * 4 + SG * SG * 8,
        ),
    )(tile_id, vis_coords, vis_values, phases)


def window_table():
    cs = jnp.arange(SG, dtype=jnp.int32)
    xs = jnp.arange(FS, dtype=jnp.int32)
    angle = ((cs[:, None] * xs[None, :]) % SG).astype(jnp.float32) * (2.0 * math.pi / SG)
    scale = 1.0 / math.sqrt(SG)
    cosine = jnp.cos(angle) * scale
    sine = jnp.sin(angle) * scale
    return jnp.concatenate(
        [jnp.concatenate([cosine, -sine], 1), jnp.concatenate([sine, cosine], 1)], 0
    )


def body(
    vis_coords,
    vis_values,
    block_dest,
    block_local,
    block_tile,
    block_counts,
    facet_offsets,
    correction,
):
    n_tm = lax.axis_size("tm")
    n_sub = lax.axis_size("sub")
    devices = n_tm * n_sub
    blocks = vis_coords.shape[0]
    band_rows = SG // n_sub
    band_tiles = band_rows // PATCH
    col_tiles = SG // PATCH
    tiles_all = col_tiles * col_tiles
    chunk = SG // devices
    facet_rows = FS // n_sub

    live = jnp.arange(blocks, dtype=jnp.int32) < block_counts[0]
    target = block_dest[:, 0]
    row_tile = (target % n_sub) * band_tiles + block_tile // col_tiles
    core = lax.axis_index("tm") % 2
    row_tile = (row_tile + core * (col_tiles // 2)) % col_tiles
    tile_id = row_tile * col_tiles + block_tile % col_tiles
    grid = make_phased_grid(vis_coords, vis_values, live, block_local, tile_id)

    pair = [(i, i ^ 1) for i in range(n_tm)]
    chip_half = grid[: SG // 2] + lax.ppermute(grid[SG // 2 :], "tm", pair)
    half_chunk = chunk // 2
    arrived = lax.all_to_all(
        chip_half.reshape(devices, half_chunk, 2, SG),
        ("tm", "sub"),
        split_axis=0,
        concat_axis=0,
        tiled=True,
    )
    grid_rows = jnp.sum(
        arrived.reshape(n_tm // 2, 2, n_sub, half_chunk, 2, SG), axis=(0, 2)
    ).reshape(chunk, 2 * SG)
    offsets = jnp.clip(facet_offsets, 0, SG - FS)
    cs = jnp.arange(SG, dtype=jnp.int32)
    shift = ((offsets[:, 1][:, None] * cs[None, :]) % SG).astype(jnp.float32) * (
        2.0 * math.pi / SG
    )
    cos_s = jnp.cos(shift)[:, None, :]
    sin_s = jnp.sin(shift)[:, None, :]
    g_re = grid_rows[None, :, :SG]
    g_im = grid_rows[None, :, SG:]
    shifted = jnp.concatenate(
        [g_re * cos_s + g_im * sin_s, g_im * cos_s - g_re * sin_s], axis=2
    ).reshape(n_tm * chunk, 2 * SG)
    windows = jnp.dot(shifted, window_table(), precision=lax.Precision.HIGHEST).reshape(
        n_tm, chunk, 2, FS
    )
    windows = jnp.broadcast_to(
        windows[:, None], (n_tm, n_sub, chunk, 2, FS)
    ).reshape(devices, chunk, 2, FS)
    gathered = lax.all_to_all(
        windows, ("tm", "sub"), split_axis=0, concat_axis=0, tiled=True
    ).reshape(SG, 2, FS)

    facet = lax.axis_index("tm")
    band = lax.axis_index("sub")
    first_y = offsets[facet, 0] + band * facet_rows
    ys = first_y + jnp.arange(facet_rows, dtype=jnp.int32)
    order = jnp.arange(SG, dtype=jnp.int32)
    rs = (
        ((order // half_chunk) % 2) * (SG // 2)
        + (order // chunk) * half_chunk
        + order % half_chunk
    )
    angle = ((ys[:, None] * rs[None, :]) % SG).astype(jnp.float32) * (2.0 * math.pi / SG)
    scale = 1.0 / math.sqrt(SG)
    left = jnp.concatenate([jnp.cos(angle) * scale, jnp.sin(angle) * scale], 1)
    real_part = gathered[:, 0]
    imag_part = gathered[:, 1]
    right = jnp.concatenate(
        [
            jnp.concatenate([real_part, imag_part], 1),
            jnp.concatenate([imag_part, -real_part], 1),
        ],
        0,
    )
    summed = jnp.dot(left, right, precision=lax.Precision.HIGHEST).reshape(
        1, facet_rows, 2, FS
    )
    return summed * correction[:, :, None, :]


def solution(mesh):
    in_specs = (
        P(("tm", "sub"), None, None),
        P(("tm", "sub"), None, None),
        P(("tm", "sub"), None),
        P(("tm", "sub")),
        P(("tm", "sub")),
        P(("tm", "sub")),
        P(),
        P("tm", "sub", None),
    )
    out_specs = P("tm", "sub", None, None)
    return jax.shard_map(body, mesh=mesh, in_specs=in_specs, out_specs=out_specs, check_vma=False)
```

```python
import math

import jax
import jax.numpy as jnp
from jax import lax
from jax.experimental import pallas as pl
from jax.experimental.pallas import tpu as pltpu
from jax.sharding import PartitionSpec as P

SG = 512
PATCH = 32
FS = 128
VIS = 1024
SG_PER = 16


kernel_width = 0.7
gauss_scale = -0.5 / (kernel_width * kernel_width) / math.log(2.0)


def split_bf16(x):
    high = x.astype(jnp.bfloat16)
    low = (x - high.astype(jnp.float32)).astype(jnp.bfloat16)
    return jnp.concatenate([high, low], axis=0)


def patch_kernel(place_ref, coords_ref, values_ref, phase_ref, out_ref):
    step = coords_ref.shape[0]
    cells = lax.broadcasted_iota(jnp.int32, (PATCH, 1), 0).astype(jnp.float32)
    pad = jnp.zeros((PATCH, 128 - PATCH), jnp.float32)
    half = out_ref.shape[1] // 2
    per_group = 128 // PATCH

    @pl.when(pl.program_id(0) == 0)
    def _():
        out_ref[...] = jnp.zeros_like(out_ref)

    def one_block(i, carry):
        x = coords_ref[i, 0:1, :]
        y = coords_ref[i, 1:2, :]
        rows_kernel = jnp.exp2(((x - cells) ** 2) * gauss_scale)
        cols_kernel = jnp.exp2(((y - cells) ** 2) * gauss_scale)
        weighted = jnp.concatenate(
            [cols_kernel * values_ref[i, 0:1, :], cols_kernel * values_ref[i, 1:2, :]], axis=0
        )
        both = lax.dot_general(
            split_bf16(rows_kernel),
            split_bf16(weighted),
            (((1,), (1,)), ((), ())),
            preferred_element_type=jnp.float32,
        )
        width = 2 * PATCH
        plain = (both[:PATCH, :width] + both[:PATCH, width:]) + (
            both[PATCH:, :width] + both[PATCH:, width:]
        )
        real_part = plain[:, :PATCH]
        imag_part = plain[:, PATCH:]
        phase = phase_ref[pl.ds(i, 1), :]
        cos_b = phase[:, :PATCH]
        sin_b = phase[:, PATCH:]
        phased = (
            real_part * cos_b + imag_part * sin_b,
            imag_part * cos_b - real_part * sin_b,
        )
        tile = place_ref[pl.program_id(0) * step + i]
        row_tile = tile // (SG // PATCH)
        col_tile = tile % (SG // PATCH)
        rows = pl.ds(pl.multiple_of(row_tile * PATCH, PATCH), PATCH)
        shift = (col_tile % per_group) * PATCH
        for part, values in enumerate(phased):
            start = pl.multiple_of(part * half + (col_tile // per_group) * 128, 128)
            padded = jnp.concatenate([values, pad], axis=1)
            out_ref[rows, pl.ds(start, 128)] += pltpu.roll(padded, shift, 1)
        return carry

    lax.fori_loop(0, step, one_block, 0)


def make_phased_grid(vis_coords, vis_values, live, local, tile_id):
    count = vis_coords.shape[0]
    step = 8
    phase = (jnp.arange(PATCH, dtype=jnp.int32)[None, :] * local[:, None]) % SG_PER
    angle = phase.astype(jnp.float32) * (2.0 * math.pi / SG_PER)
    keep = live.astype(jnp.float32)[:, None]
    phases = jnp.concatenate([jnp.cos(angle) * keep, jnp.sin(angle) * keep], axis=1)
    spec = pl.BlockSpec((step, 2, VIS), lambda i, place: (i, 0, 0))
    return pl.pallas_call(
        patch_kernel,
        grid_spec=pltpu.PrefetchScalarGridSpec(
            num_scalar_prefetch=1,
            grid=(count // step,),
            in_specs=[
                spec,
                spec,
                pl.BlockSpec((step, 2 * PATCH), lambda i, place: (i, 0)),
            ],
            out_specs=pl.BlockSpec((SG, 2 * SG), lambda i, place: (0, 0)),
        ),
        out_shape=jax.ShapeDtypeStruct((SG, 2 * SG), jnp.float32),
        cost_estimate=pl.CostEstimate(
            flops=count * 4 * PATCH * 4 * PATCH * VIS * 2,
            transcendentals=count * 2 * PATCH * VIS,
            bytes_accessed=count * 4 * VIS * 4 + SG * SG * 8,
        ),
    )(tile_id, vis_coords, vis_values, phases)


def window_table():
    cs = jnp.arange(SG, dtype=jnp.int32)
    xs = jnp.arange(FS, dtype=jnp.int32)
    angle = ((cs[:, None] * xs[None, :]) % SG).astype(jnp.float32) * (2.0 * math.pi / SG)
    scale = 1.0 / math.sqrt(SG)
    cosine = jnp.cos(angle) * scale
    sine = jnp.sin(angle) * scale
    return jnp.concatenate(
        [jnp.concatenate([cosine, -sine], 1), jnp.concatenate([sine, cosine], 1)], 0
    )


def body(
    vis_coords,
    vis_values,
    block_dest,
    block_local,
    block_tile,
    block_counts,
    facet_offsets,
    correction,
):
    n_tm = lax.axis_size("tm")
    n_sub = lax.axis_size("sub")
    devices = n_tm * n_sub
    blocks = vis_coords.shape[0]
    band_rows = SG // n_sub
    band_tiles = band_rows // PATCH
    col_tiles = SG // PATCH
    tiles_all = col_tiles * col_tiles
    chunk = SG // devices
    facet_rows = FS // n_sub

    live = jnp.arange(blocks, dtype=jnp.int32) < block_counts[0]
    target = block_dest[:, 0]
    row_tile = (target % n_sub) * band_tiles + block_tile // col_tiles
    core = lax.axis_index("tm") % 2
    row_tile = (row_tile + core * (col_tiles // 2)) % col_tiles
    tile_id = row_tile * col_tiles + block_tile % col_tiles
    grid = make_phased_grid(vis_coords, vis_values, live, block_local, tile_id)

    pair = [(i, i ^ 1) for i in range(n_tm)]
    chip_half = grid[: SG // 2] + lax.ppermute(grid[SG // 2 :], "tm", pair)
    half_chunk = chunk // 2
    arrived = lax.all_to_all(
        chip_half.reshape(devices, half_chunk, 2, SG),
        ("tm", "sub"),
        split_axis=0,
        concat_axis=0,
        tiled=True,
    )
    grid_rows = jnp.sum(
        arrived.reshape(n_tm // 2, 2, n_sub, half_chunk, 2, SG), axis=(0, 2)
    ).reshape(chunk, 2 * SG)
    offsets = jnp.clip(facet_offsets, 0, SG - FS)
    cs = jnp.arange(SG, dtype=jnp.int32)
    shift = ((offsets[:, 1][:, None] * cs[None, :]) % SG).astype(jnp.float32) * (
        2.0 * math.pi / SG
    )
    cos_s = jnp.cos(shift)[:, None, :]
    sin_s = jnp.sin(shift)[:, None, :]
    g_re = grid_rows[None, :, :SG]
    g_im = grid_rows[None, :, SG:]
    shifted = jnp.concatenate(
        [g_re * cos_s + g_im * sin_s, g_im * cos_s - g_re * sin_s], axis=2
    ).reshape(n_tm * chunk, 2 * SG)
    windows = jnp.dot(shifted, window_table(), precision=lax.Precision.HIGHEST).reshape(
        n_tm, chunk, 2, FS
    )
    windows = jnp.broadcast_to(
        windows[:, None], (n_tm, n_sub, chunk, 2, FS)
    ).reshape(devices, chunk, 2, FS)
    gathered = lax.all_to_all(
        windows, ("tm", "sub"), split_axis=0, concat_axis=0, tiled=True
    ).reshape(SG, 2, FS)

    facet = lax.axis_index("tm")
    band = lax.axis_index("sub")
    first_y = offsets[facet, 0] + band * facet_rows
    ys = first_y + jnp.arange(facet_rows, dtype=jnp.int32)
    order = jnp.arange(SG, dtype=jnp.int32)
    rs = (
        ((order // half_chunk) % 2) * (SG // 2)
        + (order // chunk) * half_chunk
        + order % half_chunk
    )
    angle = ((ys[:, None] * rs[None, :]) % SG).astype(jnp.float32) * (2.0 * math.pi / SG)
    scale = 1.0 / math.sqrt(SG)
    left = jnp.concatenate([jnp.cos(angle) * scale, jnp.sin(angle) * scale], 1)
    real_part = gathered[:, 0]
    imag_part = gathered[:, 1]
    right = jnp.concatenate(
        [
            jnp.concatenate([real_part, imag_part], 1),
            jnp.concatenate([imag_part, -real_part], 1),
        ],
        0,
    )
    summed = jnp.dot(left, right, precision=lax.Precision.HIGHEST).reshape(
        1, facet_rows, 2, FS
    )
    return summed * correction[:, :, None, :]


def solution(mesh):
    in_specs = (
        P(("tm", "sub"), None, None),
        P(("tm", "sub"), None, None),
        P(("tm", "sub"), None),
        P(("tm", "sub")),
        P(("tm", "sub")),
        P(("tm", "sub")),
        P(),
        P("tm", "sub", None),
    )
    out_specs = P("tm", "sub", None, None)
    return jax.shard_map(body, mesh=mesh, in_specs=in_specs, out_specs=out_specs, check_vma=False)
```

```python
import math

import jax
import jax.numpy as jnp
from jax import lax
from jax.experimental import pallas as pl
from jax.experimental.pallas import tpu as pltpu
from jax.sharding import PartitionSpec as P

SG = 512
PATCH = 32
FS = 128
VIS = 1024
SG_PER = 16


kernel_width = 0.7
gauss_scale = -0.5 / (kernel_width * kernel_width) / math.log(2.0)


def split_bf16(x):
    high = x.astype(jnp.bfloat16)
    low = (x - high.astype(jnp.float32)).astype(jnp.bfloat16)
    return jnp.concatenate([high, low], axis=0)


def patch_kernel(place_ref, coords_ref, values_ref, phase_ref, out_ref):
    step = coords_ref.shape[0]
    width = 2 * PATCH
    cells = lax.broadcasted_iota(jnp.int32, (PATCH, 1), 0).astype(jnp.float32)
    lane_half = lax.broadcasted_iota(jnp.int32, (PATCH, 2 * width), 1) // width

    @pl.when(pl.program_id(0) == 0)
    def _():
        out_ref[...] = jnp.zeros_like(out_ref)

    def one_block(i, carry):
        x = coords_ref[i, 0:1, :]
        y = coords_ref[i, 1:2, :]
        rows_kernel = jnp.exp2(((x - cells) ** 2) * gauss_scale)
        cols_kernel = jnp.exp2(((y - cells) ** 2) * gauss_scale)
        weighted = jnp.concatenate(
            [cols_kernel * values_ref[i, 0:1, :], cols_kernel * values_ref[i, 1:2, :]], axis=0
        )
        both = lax.dot_general(
            split_bf16(rows_kernel),
            split_bf16(weighted),
            (((1,), (1,)), ((), ())),
            preferred_element_type=jnp.float32,
        )
        both = both + pltpu.roll(both, width, 1)
        plain = both[:PATCH] + both[PATCH:]
        swapped = pltpu.roll(plain, PATCH, 1)
        phase = phase_ref[pl.ds(i, 1), :]
        phased = plain * phase[:, : 2 * width] + swapped * phase[:, 2 * width :]
        tile = place_ref[pl.program_id(0) * step + i]
        row_tile = tile // (SG // PATCH)
        col_tile = tile % (SG // PATCH)
        rows = pl.ds(pl.multiple_of(row_tile * PATCH, PATCH), PATCH)
        start = pl.multiple_of((col_tile // 2) * 2 * width, 2 * width)
        out_ref[rows, pl.ds(start, 2 * width)] += jnp.where(
            lane_half == col_tile % 2, phased, 0.0
        )
        return carry

    lax.fori_loop(0, step, one_block, 0)


def make_phased_grid(vis_coords, vis_values, live, local, tile_id):
    count = vis_coords.shape[0]
    step = 8
    phase = (jnp.arange(PATCH, dtype=jnp.int32)[None, :] * local[:, None]) % SG_PER
    angle = phase.astype(jnp.float32) * (2.0 * math.pi / SG_PER)
    keep = live.astype(jnp.float32)[:, None]
    cos_b = jnp.cos(angle) * keep
    sin_b = jnp.sin(angle) * keep
    phases = jnp.concatenate(
        [cos_b, cos_b, cos_b, cos_b, sin_b, -sin_b, sin_b, -sin_b], axis=1
    )
    spec = pl.BlockSpec((step, 2, VIS), lambda i, place: (i, 0, 0))
    return pl.pallas_call(
        patch_kernel,
        grid_spec=pltpu.PrefetchScalarGridSpec(
            num_scalar_prefetch=1,
            grid=(count // step,),
            in_specs=[
                spec,
                spec,
                pl.BlockSpec((step, 8 * PATCH), lambda i, place: (i, 0)),
            ],
            out_specs=pl.BlockSpec((SG, 2 * SG), lambda i, place: (0, 0)),
        ),
        out_shape=jax.ShapeDtypeStruct((SG, 2 * SG), jnp.float32),
        cost_estimate=pl.CostEstimate(
            flops=count * 4 * PATCH * 4 * PATCH * VIS * 2,
            transcendentals=count * 2 * PATCH * VIS,
            bytes_accessed=count * 4 * VIS * 4 + SG * SG * 8,
        ),
    )(tile_id, vis_coords, vis_values, phases)


def window_table():
    cs = jnp.arange(SG, dtype=jnp.int32)
    xs = jnp.arange(FS, dtype=jnp.int32)
    angle = ((cs[:, None] * xs[None, :]) % SG).astype(jnp.float32) * (2.0 * math.pi / SG)
    scale = 1.0 / math.sqrt(SG)
    cosine = jnp.cos(angle) * scale
    sine = jnp.sin(angle) * scale
    return jnp.concatenate(
        [jnp.concatenate([cosine, -sine], 1), jnp.concatenate([sine, cosine], 1)], 0
    )


def body(
    vis_coords,
    vis_values,
    block_dest,
    block_local,
    block_tile,
    block_counts,
    facet_offsets,
    correction,
):
    n_tm = lax.axis_size("tm")
    n_sub = lax.axis_size("sub")
    devices = n_tm * n_sub
    blocks = vis_coords.shape[0]
    band_rows = SG // n_sub
    band_tiles = band_rows // PATCH
    col_tiles = SG // PATCH
    tiles_all = col_tiles * col_tiles
    chunk = SG // devices
    facet_rows = FS // n_sub

    live = jnp.arange(blocks, dtype=jnp.int32) < block_counts[0]
    target = block_dest[:, 0]
    row_tile = (target % n_sub) * band_tiles + block_tile // col_tiles
    core = lax.axis_index("tm") % 2
    row_tile = (row_tile + core * (col_tiles // 2)) % col_tiles
    tile_id = row_tile * col_tiles + block_tile % col_tiles
    grid = make_phased_grid(vis_coords, vis_values, live, block_local, tile_id)

    pair = [(i, i ^ 1) for i in range(n_tm)]
    chip_half = grid[: SG // 2] + lax.ppermute(grid[SG // 2 :], "tm", pair)
    half_chunk = chunk // 2
    arrived = lax.all_to_all(
        chip_half.reshape(devices, half_chunk, 2, SG),
        ("tm", "sub"),
        split_axis=0,
        concat_axis=0,
        tiled=True,
    )
    grid_rows = jnp.sum(
        arrived.reshape(n_tm // 2, 2, n_sub, half_chunk, 2, SG), axis=(0, 2)
    )
    grid_rows = (
        grid_rows.reshape(chunk, col_tiles, 2, PATCH).transpose(0, 2, 1, 3).reshape(chunk, 2 * SG)
    )
    offsets = jnp.clip(facet_offsets, 0, SG - FS)
    cs = jnp.arange(SG, dtype=jnp.int32)
    shift = ((offsets[:, 1][:, None] * cs[None, :]) % SG).astype(jnp.float32) * (
        2.0 * math.pi / SG
    )
    cos_s = jnp.cos(shift)[:, None, :]
    sin_s = jnp.sin(shift)[:, None, :]
    g_re = grid_rows[None, :, :SG]
    g_im = grid_rows[None, :, SG:]
    shifted = jnp.concatenate(
        [g_re * cos_s + g_im * sin_s, g_im * cos_s - g_re * sin_s], axis=2
    ).reshape(n_tm * chunk, 2 * SG)
    windows = jnp.dot(shifted, window_table(), precision=lax.Precision.HIGHEST).reshape(
        n_tm, chunk, 2, FS
    )
    windows = jnp.broadcast_to(
        windows[:, None], (n_tm, n_sub, chunk, 2, FS)
    ).reshape(devices, chunk, 2, FS)
    gathered = lax.all_to_all(
        windows, ("tm", "sub"), split_axis=0, concat_axis=0, tiled=True
    ).reshape(SG, 2, FS)

    facet = lax.axis_index("tm")
    band = lax.axis_index("sub")
    first_y = offsets[facet, 0] + band * facet_rows
    ys = first_y + jnp.arange(facet_rows, dtype=jnp.int32)
    order = jnp.arange(SG, dtype=jnp.int32)
    rs = (
        ((order // half_chunk) % 2) * (SG // 2)
        + (order // chunk) * half_chunk
        + order % half_chunk
    )
    angle = ((ys[:, None] * rs[None, :]) % SG).astype(jnp.float32) * (2.0 * math.pi / SG)
    scale = 1.0 / math.sqrt(SG)
    left = jnp.concatenate([jnp.cos(angle) * scale, jnp.sin(angle) * scale], 1)
    real_part = gathered[:, 0]
    imag_part = gathered[:, 1]
    right = jnp.concatenate(
        [
            jnp.concatenate([real_part, imag_part], 1),
            jnp.concatenate([imag_part, -real_part], 1),
        ],
        0,
    )
    summed = jnp.dot(left, right, precision=lax.Precision.HIGHEST).reshape(
        1, facet_rows, 2, FS
    )
    return summed * correction[:, :, None, :]


def solution(mesh):
    in_specs = (
        P(("tm", "sub"), None, None),
        P(("tm", "sub"), None, None),
        P(("tm", "sub"), None),
        P(("tm", "sub")),
        P(("tm", "sub")),
        P(("tm", "sub")),
        P(),
        P("tm", "sub", None),
    )
    out_specs = P("tm", "sub", None, None)
    return jax.shard_map(body, mesh=mesh, in_specs=in_specs, out_specs=out_specs, check_vma=False)
```

```python
import math

import jax
import jax.numpy as jnp
from jax import lax
from jax.experimental import pallas as pl
from jax.experimental.pallas import tpu as pltpu
from jax.sharding import PartitionSpec as P

SG = 512
PATCH = 32
FS = 128
VIS = 1024
SG_PER = 16


kernel_width = 0.7
gauss_scale = -0.5 / (kernel_width * kernel_width) / math.log(2.0)


def split_bf16(x):
    high = x.astype(jnp.bfloat16)
    low = (x - high.astype(jnp.float32)).astype(jnp.bfloat16)
    return jnp.concatenate([high, low], axis=0)


def patch_kernel(place_ref, coords_ref, values_ref, phase_ref, out_ref):
    step = coords_ref.shape[0]
    width = 2 * PATCH
    cells = lax.broadcasted_iota(jnp.int32, (PATCH, 1), 0).astype(jnp.float32)
    lane_half = lax.broadcasted_iota(jnp.int32, (PATCH, 2 * width), 1) // width

    @pl.when(pl.program_id(0) == 0)
    def _():
        out_ref[...] = jnp.zeros_like(out_ref)

    def one_block(i, carry):
        x = coords_ref[i, 0:1, :]
        y = coords_ref[i, 1:2, :]
        rows_kernel = jnp.exp2(((x - cells) ** 2) * gauss_scale)
        cols_kernel = jnp.exp2(((y - cells) ** 2) * gauss_scale)
        weighted = jnp.concatenate(
            [cols_kernel * values_ref[i, 0:1, :], cols_kernel * values_ref[i, 1:2, :]], axis=0
        )
        both = lax.dot_general(
            split_bf16(rows_kernel),
            split_bf16(weighted),
            (((1,), (1,)), ((), ())),
            preferred_element_type=jnp.float32,
        )
        both = both + pltpu.roll(both, width, 1)
        plain = both[:PATCH] + both[PATCH:]
        swapped = pltpu.roll(plain, PATCH, 1)
        phase = phase_ref[pl.ds(i, 1), :]
        phased = plain * phase[:, : 2 * width] + swapped * phase[:, 2 * width :]
        tile = place_ref[pl.program_id(0) * step + i]
        row_tile = tile // (SG // PATCH)
        col_tile = tile % (SG // PATCH)
        rows = pl.ds(pl.multiple_of(row_tile * PATCH, PATCH), PATCH)
        start = pl.multiple_of((col_tile // 2) * 2 * width, 2 * width)
        out_ref[rows, pl.ds(start, 2 * width)] += jnp.where(
            lane_half == col_tile % 2, phased, 0.0
        )
        return carry

    lax.fori_loop(0, step, one_block, 0)


def make_phased_grid(vis_coords, vis_values, live, local, tile_id):
    count = vis_coords.shape[0]
    step = 32
    phase = (jnp.arange(PATCH, dtype=jnp.int32)[None, :] * local[:, None]) % SG_PER
    angle = phase.astype(jnp.float32) * (2.0 * math.pi / SG_PER)
    keep = live.astype(jnp.float32)[:, None]
    cos_b = jnp.cos(angle) * keep
    sin_b = jnp.sin(angle) * keep
    phases = jnp.concatenate(
        [cos_b, cos_b, cos_b, cos_b, sin_b, -sin_b, sin_b, -sin_b], axis=1
    )
    spec = pl.BlockSpec((step, 2, VIS), lambda i, place: (i, 0, 0))
    return pl.pallas_call(
        patch_kernel,
        grid_spec=pltpu.PrefetchScalarGridSpec(
            num_scalar_prefetch=1,
            grid=(count // step,),
            in_specs=[
                spec,
                spec,
                pl.BlockSpec((step, 8 * PATCH), lambda i, place: (i, 0)),
            ],
            out_specs=pl.BlockSpec((SG, 2 * SG), lambda i, place: (0, 0)),
        ),
        out_shape=jax.ShapeDtypeStruct((SG, 2 * SG), jnp.float32),
        cost_estimate=pl.CostEstimate(
            flops=count * 4 * PATCH * 4 * PATCH * VIS * 2,
            transcendentals=count * 2 * PATCH * VIS,
            bytes_accessed=count * 4 * VIS * 4 + SG * SG * 8,
        ),
    )(tile_id, vis_coords, vis_values, phases)


def window_table():
    cs = jnp.arange(SG, dtype=jnp.int32)
    xs = jnp.arange(FS, dtype=jnp.int32)
    angle = ((cs[:, None] * xs[None, :]) % SG).astype(jnp.float32) * (2.0 * math.pi / SG)
    scale = 1.0 / math.sqrt(SG)
    cosine = jnp.cos(angle) * scale
    sine = jnp.sin(angle) * scale
    return jnp.concatenate(
        [jnp.concatenate([cosine, -sine], 1), jnp.concatenate([sine, cosine], 1)], 0
    )


def body(
    vis_coords,
    vis_values,
    block_dest,
    block_local,
    block_tile,
    block_counts,
    facet_offsets,
    correction,
):
    n_tm = lax.axis_size("tm")
    n_sub = lax.axis_size("sub")
    devices = n_tm * n_sub
    blocks = vis_coords.shape[0]
    band_rows = SG // n_sub
    band_tiles = band_rows // PATCH
    col_tiles = SG // PATCH
    tiles_all = col_tiles * col_tiles
    chunk = SG // devices
    facet_rows = FS // n_sub

    live = jnp.arange(blocks, dtype=jnp.int32) < block_counts[0]
    target = block_dest[:, 0]
    row_tile = (target % n_sub) * band_tiles + block_tile // col_tiles
    core = lax.axis_index("tm") % 2
    row_tile = (row_tile + core * (col_tiles // 2)) % col_tiles
    tile_id = row_tile * col_tiles + block_tile % col_tiles
    grid = make_phased_grid(vis_coords, vis_values, live, block_local, tile_id)

    pair = [(i, i ^ 1) for i in range(n_tm)]
    chip_half = grid[: SG // 2] + lax.ppermute(grid[SG // 2 :], "tm", pair)
    half_chunk = chunk // 2
    arrived = lax.all_to_all(
        chip_half.reshape(devices, half_chunk, 2, SG),
        ("tm", "sub"),
        split_axis=0,
        concat_axis=0,
        tiled=True,
    )
    grid_rows = jnp.sum(
        arrived.reshape(n_tm // 2, 2, n_sub, half_chunk, 2, SG), axis=(0, 2)
    )
    grid_rows = (
        grid_rows.reshape(chunk, col_tiles, 2, PATCH).transpose(0, 2, 1, 3).reshape(chunk, 2 * SG)
    )
    offsets = jnp.clip(facet_offsets, 0, SG - FS)
    cs = jnp.arange(SG, dtype=jnp.int32)
    shift = ((offsets[:, 1][:, None] * cs[None, :]) % SG).astype(jnp.float32) * (
        2.0 * math.pi / SG
    )
    cos_s = jnp.cos(shift)[:, None, :]
    sin_s = jnp.sin(shift)[:, None, :]
    g_re = grid_rows[None, :, :SG]
    g_im = grid_rows[None, :, SG:]
    shifted = jnp.concatenate(
        [g_re * cos_s + g_im * sin_s, g_im * cos_s - g_re * sin_s], axis=2
    ).reshape(n_tm * chunk, 2 * SG)
    windows = jnp.dot(shifted, window_table(), precision=lax.Precision.HIGHEST).reshape(
        n_tm, chunk, 2, FS
    )
    windows = jnp.broadcast_to(
        windows[:, None], (n_tm, n_sub, chunk, 2, FS)
    ).reshape(devices, chunk, 2, FS)
    gathered = lax.all_to_all(
        windows, ("tm", "sub"), split_axis=0, concat_axis=0, tiled=True
    ).reshape(SG, 2, FS)

    facet = lax.axis_index("tm")
    band = lax.axis_index("sub")
    first_y = offsets[facet, 0] + band * facet_rows
    ys = first_y + jnp.arange(facet_rows, dtype=jnp.int32)
    order = jnp.arange(SG, dtype=jnp.int32)
    rs = (
        ((order // half_chunk) % 2) * (SG // 2)
        + (order // chunk) * half_chunk
        + order % half_chunk
    )
    angle = ((ys[:, None] * rs[None, :]) % SG).astype(jnp.float32) * (2.0 * math.pi / SG)
    scale = 1.0 / math.sqrt(SG)
    left = jnp.concatenate([jnp.cos(angle) * scale, jnp.sin(angle) * scale], 1)
    real_part = gathered[:, 0]
    imag_part = gathered[:, 1]
    right = jnp.concatenate(
        [
            jnp.concatenate([real_part, imag_part], 1),
            jnp.concatenate([imag_part, -real_part], 1),
        ],
        0,
    )
    summed = jnp.dot(left, right, precision=lax.Precision.HIGHEST).reshape(
        1, facet_rows, 2, FS
    )
    return summed * correction[:, :, None, :]


def solution(mesh):
    in_specs = (
        P(("tm", "sub"), None, None),
        P(("tm", "sub"), None, None),
        P(("tm", "sub"), None),
        P(("tm", "sub")),
        P(("tm", "sub")),
        P(("tm", "sub")),
        P(),
        P("tm", "sub", None),
    )
    out_specs = P("tm", "sub", None, None)
    return jax.shard_map(body, mesh=mesh, in_specs=in_specs, out_specs=out_specs, check_vma=False)
```

```python
import math

import jax
import jax.numpy as jnp
from jax import lax
from jax.experimental import pallas as pl
from jax.experimental.pallas import tpu as pltpu
from jax.sharding import PartitionSpec as P

SG = 512
PATCH = 32
FS = 128
VIS = 1024
SG_PER = 16


kernel_width = 0.7
gauss_scale = -0.5 / (kernel_width * kernel_width) / math.log(2.0)


def split_bf16(x):
    high = x.astype(jnp.bfloat16)
    low = (x - high.astype(jnp.float32)).astype(jnp.bfloat16)
    return jnp.concatenate([high, low], axis=0)


def patch_kernel(place_ref, coords_ref, values_ref, phase_ref, out_ref):
    step = coords_ref.shape[0]
    width = 2 * PATCH
    cells = lax.broadcasted_iota(jnp.int32, (PATCH, 1), 0).astype(jnp.float32)
    lane_half = lax.broadcasted_iota(jnp.int32, (PATCH, 2 * width), 1) // width

    @pl.when(pl.program_id(0) == 0)
    def _():
        out_ref[...] = jnp.zeros_like(out_ref)

    def one_block(i, carry):
        x = coords_ref[i, 0:1, :]
        y = coords_ref[i, 1:2, :]
        rows_kernel = jnp.exp2(((x - cells) ** 2) * gauss_scale)
        cols_kernel = jnp.exp2(((y - cells) ** 2) * gauss_scale)
        weighted = jnp.concatenate(
            [cols_kernel * values_ref[i, 0:1, :], cols_kernel * values_ref[i, 1:2, :]], axis=0
        )
        both = lax.dot_general(
            split_bf16(rows_kernel),
            split_bf16(weighted),
            (((1,), (1,)), ((), ())),
            preferred_element_type=jnp.float32,
        )
        both = both + pltpu.roll(both, width, 1)
        plain = both[:PATCH] + both[PATCH:]
        swapped = pltpu.roll(plain, PATCH, 1)
        phase = phase_ref[pl.ds(i, 1), :]
        phased = plain * phase[:, : 2 * width] + swapped * phase[:, 2 * width :]
        tile = place_ref[pl.program_id(0) * step + i]
        row_tile = tile // (SG // PATCH)
        col_tile = tile % (SG // PATCH)
        rows = pl.ds(pl.multiple_of(row_tile * PATCH, PATCH), PATCH)
        start = pl.multiple_of((col_tile // 2) * 2 * width, 2 * width)
        out_ref[rows, pl.ds(start, 2 * width)] += jnp.where(
            lane_half == col_tile % 2, phased, 0.0
        )
        return carry

    lax.fori_loop(0, step, one_block, 0, unroll=2)


def make_phased_grid(vis_coords, vis_values, live, local, tile_id):
    count = vis_coords.shape[0]
    step = 8
    phase = (jnp.arange(PATCH, dtype=jnp.int32)[None, :] * local[:, None]) % SG_PER
    angle = phase.astype(jnp.float32) * (2.0 * math.pi / SG_PER)
    keep = live.astype(jnp.float32)[:, None]
    cos_b = jnp.cos(angle) * keep
    sin_b = jnp.sin(angle) * keep
    phases = jnp.concatenate(
        [cos_b, cos_b, cos_b, cos_b, sin_b, -sin_b, sin_b, -sin_b], axis=1
    )
    spec = pl.BlockSpec((step, 2, VIS), lambda i, place: (i, 0, 0))
    return pl.pallas_call(
        patch_kernel,
        grid_spec=pltpu.PrefetchScalarGridSpec(
            num_scalar_prefetch=1,
            grid=(count // step,),
            in_specs=[
                spec,
                spec,
                pl.BlockSpec((step, 8 * PATCH), lambda i, place: (i, 0)),
            ],
            out_specs=pl.BlockSpec((SG, 2 * SG), lambda i, place: (0, 0)),
        ),
        out_shape=jax.ShapeDtypeStruct((SG, 2 * SG), jnp.float32),
        cost_estimate=pl.CostEstimate(
            flops=count * 4 * PATCH * 4 * PATCH * VIS * 2,
            transcendentals=count * 2 * PATCH * VIS,
            bytes_accessed=count * 4 * VIS * 4 + SG * SG * 8,
        ),
    )(tile_id, vis_coords, vis_values, phases)


def window_table():
    cs = jnp.arange(SG, dtype=jnp.int32)
    xs = jnp.arange(FS, dtype=jnp.int32)
    angle = ((cs[:, None] * xs[None, :]) % SG).astype(jnp.float32) * (2.0 * math.pi / SG)
    scale = 1.0 / math.sqrt(SG)
    cosine = jnp.cos(angle) * scale
    sine = jnp.sin(angle) * scale
    return jnp.concatenate(
        [jnp.concatenate([cosine, -sine], 1), jnp.concatenate([sine, cosine], 1)], 0
    )


def body(
    vis_coords,
    vis_values,
    block_dest,
    block_local,
    block_tile,
    block_counts,
    facet_offsets,
    correction,
):
    n_tm = lax.axis_size("tm")
    n_sub = lax.axis_size("sub")
    devices = n_tm * n_sub
    blocks = vis_coords.shape[0]
    band_rows = SG // n_sub
    band_tiles = band_rows // PATCH
    col_tiles = SG // PATCH
    tiles_all = col_tiles * col_tiles
    chunk = SG // devices
    facet_rows = FS // n_sub

    live = jnp.arange(blocks, dtype=jnp.int32) < block_counts[0]
    target = block_dest[:, 0]
    row_tile = (target % n_sub) * band_tiles + block_tile // col_tiles
    core = lax.axis_index("tm") % 2
    row_tile = (row_tile + core * (col_tiles // 2)) % col_tiles
    tile_id = row_tile * col_tiles + block_tile % col_tiles
    grid = make_phased_grid(vis_coords, vis_values, live, block_local, tile_id)

    pair = [(i, i ^ 1) for i in range(n_tm)]
    chip_half = grid[: SG // 2] + lax.ppermute(grid[SG // 2 :], "tm", pair)
    half_chunk = chunk // 2
    arrived = lax.all_to_all(
        chip_half.reshape(devices, half_chunk, 2, SG),
        ("tm", "sub"),
        split_axis=0,
        concat_axis=0,
        tiled=True,
    )
    grid_rows = jnp.sum(
        arrived.reshape(n_tm // 2, 2, n_sub, half_chunk, 2, SG), axis=(0, 2)
    )
    grid_rows = (
        grid_rows.reshape(chunk, col_tiles, 2, PATCH).transpose(0, 2, 1, 3).reshape(chunk, 2 * SG)
    )
    offsets = jnp.clip(facet_offsets, 0, SG - FS)
    cs = jnp.arange(SG, dtype=jnp.int32)
    shift = ((offsets[:, 1][:, None] * cs[None, :]) % SG).astype(jnp.float32) * (
        2.0 * math.pi / SG
    )
    cos_s = jnp.cos(shift)[:, None, :]
    sin_s = jnp.sin(shift)[:, None, :]
    g_re = grid_rows[None, :, :SG]
    g_im = grid_rows[None, :, SG:]
    shifted = jnp.concatenate(
        [g_re * cos_s + g_im * sin_s, g_im * cos_s - g_re * sin_s], axis=2
    ).reshape(n_tm * chunk, 2 * SG)
    windows = jnp.dot(shifted, window_table(), precision=lax.Precision.HIGHEST).reshape(
        n_tm, chunk, 2, FS
    )
    windows = jnp.broadcast_to(
        windows[:, None], (n_tm, n_sub, chunk, 2, FS)
    ).reshape(devices, chunk, 2, FS)
    gathered = lax.all_to_all(
        windows, ("tm", "sub"), split_axis=0, concat_axis=0, tiled=True
    ).reshape(SG, 2, FS)

    facet = lax.axis_index("tm")
    band = lax.axis_index("sub")
    first_y = offsets[facet, 0] + band * facet_rows
    ys = first_y + jnp.arange(facet_rows, dtype=jnp.int32)
    order = jnp.arange(SG, dtype=jnp.int32)
    rs = (
        ((order // half_chunk) % 2) * (SG // 2)
        + (order // chunk) * half_chunk
        + order % half_chunk
    )
    angle = ((ys[:, None] * rs[None, :]) % SG).astype(jnp.float32) * (2.0 * math.pi / SG)
    scale = 1.0 / math.sqrt(SG)
    left = jnp.concatenate([jnp.cos(angle) * scale, jnp.sin(angle) * scale], 1)
    real_part = gathered[:, 0]
    imag_part = gathered[:, 1]
    right = jnp.concatenate(
        [
            jnp.concatenate([real_part, imag_part], 1),
            jnp.concatenate([imag_part, -real_part], 1),
        ],
        0,
    )
    summed = jnp.dot(left, right, precision=lax.Precision.HIGHEST).reshape(
        1, facet_rows, 2, FS
    )
    return summed * correction[:, :, None, :]


def solution(mesh):
    in_specs = (
        P(("tm", "sub"), None, None),
        P(("tm", "sub"), None, None),
        P(("tm", "sub"), None),
        P(("tm", "sub")),
        P(("tm", "sub")),
        P(("tm", "sub")),
        P(),
        P("tm", "sub", None),
    )
    out_specs = P("tm", "sub", None, None)
    return jax.shard_map(body, mesh=mesh, in_specs=in_specs, out_specs=out_specs, check_vma=False)
```

```python
import math

import jax
import jax.numpy as jnp
from jax import lax
from jax.experimental import pallas as pl
from jax.experimental.pallas import tpu as pltpu
from jax.sharding import PartitionSpec as P

SG = 512
PATCH = 32
FS = 128
VIS = 1024
SG_PER = 16


kernel_width = 0.7
gauss_scale = -0.5 / (kernel_width * kernel_width) / math.log(2.0)


def split_bf16(x):
    high = x.astype(jnp.bfloat16)
    low = (x - high.astype(jnp.float32)).astype(jnp.bfloat16)
    return jnp.concatenate([high, low], axis=0)


def patch_kernel(place_ref, coords_ref, values_ref, phase_ref, out_ref):
    step = coords_ref.shape[0]
    width = 2 * PATCH
    cells = lax.broadcasted_iota(jnp.int32, (PATCH, 1), 0).astype(jnp.float32)
    lane_half = lax.broadcasted_iota(jnp.int32, (PATCH, 2 * width), 1) // width

    @pl.when(pl.program_id(0) == 0)
    def _():
        out_ref[...] = jnp.zeros_like(out_ref)

    def one_block(i, carry):
        x = coords_ref[i, 0:1, :]
        y = coords_ref[i, 1:2, :]
        rows_kernel = jnp.exp2(((x - cells) ** 2) * gauss_scale)
        cols_kernel = jnp.exp2(((y - cells) ** 2) * gauss_scale)
        weighted = jnp.concatenate(
            [cols_kernel * values_ref[i, 0:1, :], cols_kernel * values_ref[i, 1:2, :]], axis=0
        )
        both = lax.dot_general(
            split_bf16(rows_kernel),
            split_bf16(weighted),
            (((1,), (1,)), ((), ())),
            preferred_element_type=jnp.float32,
        )
        both = both + pltpu.roll(both, width, 1)
        plain = both[:PATCH] + both[PATCH:]
        swapped = pltpu.roll(plain, PATCH, 1)
        phase = phase_ref[pl.ds(i, 1), :]
        phased = plain * phase[:, : 2 * width] + swapped * phase[:, 2 * width :]
        tile = place_ref[pl.program_id(0) * step + i]
        row_tile = tile // (SG // PATCH)
        col_tile = tile % (SG // PATCH)
        rows = pl.ds(pl.multiple_of(row_tile * PATCH, PATCH), PATCH)
        start = pl.multiple_of((col_tile // 2) * 2 * width, 2 * width)
        out_ref[rows, pl.ds(start, 2 * width)] += jnp.where(
            lane_half == col_tile % 2, phased, 0.0
        )
        return carry

    lax.fori_loop(0, step, one_block, 0, unroll=4)


def make_phased_grid(vis_coords, vis_values, live, local, tile_id):
    count = vis_coords.shape[0]
    step = 8
    phase = (jnp.arange(PATCH, dtype=jnp.int32)[None, :] * local[:, None]) % SG_PER
    angle = phase.astype(jnp.float32) * (2.0 * math.pi / SG_PER)
    keep = live.astype(jnp.float32)[:, None]
    cos_b = jnp.cos(angle) * keep
    sin_b = jnp.sin(angle) * keep
    phases = jnp.concatenate(
        [cos_b, cos_b, cos_b, cos_b, sin_b, -sin_b, sin_b, -sin_b], axis=1
    )
    spec = pl.BlockSpec((step, 2, VIS), lambda i, place: (i, 0, 0))
    return pl.pallas_call(
        patch_kernel,
        grid_spec=pltpu.PrefetchScalarGridSpec(
            num_scalar_prefetch=1,
            grid=(count // step,),
            in_specs=[
                spec,
                spec,
                pl.BlockSpec((step, 8 * PATCH), lambda i, place: (i, 0)),
            ],
            out_specs=pl.BlockSpec((SG, 2 * SG), lambda i, place: (0, 0)),
        ),
        out_shape=jax.ShapeDtypeStruct((SG, 2 * SG), jnp.float32),
        cost_estimate=pl.CostEstimate(
            flops=count * 4 * PATCH * 4 * PATCH * VIS * 2,
            transcendentals=count * 2 * PATCH * VIS,
            bytes_accessed=count * 4 * VIS * 4 + SG * SG * 8,
        ),
    )(tile_id, vis_coords, vis_values, phases)


def window_table():
    cs = jnp.arange(SG, dtype=jnp.int32)
    xs = jnp.arange(FS, dtype=jnp.int32)
    angle = ((cs[:, None] * xs[None, :]) % SG).astype(jnp.float32) * (2.0 * math.pi / SG)
    scale = 1.0 / math.sqrt(SG)
    cosine = jnp.cos(angle) * scale
    sine = jnp.sin(angle) * scale
    return jnp.concatenate(
        [jnp.concatenate([cosine, -sine], 1), jnp.concatenate([sine, cosine], 1)], 0
    )


def body(
    vis_coords,
    vis_values,
    block_dest,
    block_local,
    block_tile,
    block_counts,
    facet_offsets,
    correction,
):
    n_tm = lax.axis_size("tm")
    n_sub = lax.axis_size("sub")
    devices = n_tm * n_sub
    blocks = vis_coords.shape[0]
    band_rows = SG // n_sub
    band_tiles = band_rows // PATCH
    col_tiles = SG // PATCH
    tiles_all = col_tiles * col_tiles
    chunk = SG // devices
    facet_rows = FS // n_sub

    live = jnp.arange(blocks, dtype=jnp.int32) < block_counts[0]
    target = block_dest[:, 0]
    row_tile = (target % n_sub) * band_tiles + block_tile // col_tiles
    core = lax.axis_index("tm") % 2
    row_tile = (row_tile + core * (col_tiles // 2)) % col_tiles
    tile_id = row_tile * col_tiles + block_tile % col_tiles
    grid = make_phased_grid(vis_coords, vis_values, live, block_local, tile_id)

    pair = [(i, i ^ 1) for i in range(n_tm)]
    chip_half = grid[: SG // 2] + lax.ppermute(grid[SG // 2 :], "tm", pair)
    half_chunk = chunk // 2
    arrived = lax.all_to_all(
        chip_half.reshape(devices, half_chunk, 2, SG),
        ("tm", "sub"),
        split_axis=0,
        concat_axis=0,
        tiled=True,
    )
    grid_rows = jnp.sum(
        arrived.reshape(n_tm // 2, 2, n_sub, half_chunk, 2, SG), axis=(0, 2)
    )
    grid_rows = (
        grid_rows.reshape(chunk, col_tiles, 2, PATCH).transpose(0, 2, 1, 3).reshape(chunk, 2 * SG)
    )
    offsets = jnp.clip(facet_offsets, 0, SG - FS)
    cs = jnp.arange(SG, dtype=jnp.int32)
    shift = ((offsets[:, 1][:, None] * cs[None, :]) % SG).astype(jnp.float32) * (
        2.0 * math.pi / SG
    )
    cos_s = jnp.cos(shift)[:, None, :]
    sin_s = jnp.sin(shift)[:, None, :]
    g_re = grid_rows[None, :, :SG]
    g_im = grid_rows[None, :, SG:]
    shifted = jnp.concatenate(
        [g_re * cos_s + g_im * sin_s, g_im * cos_s - g_re * sin_s], axis=2
    ).reshape(n_tm * chunk, 2 * SG)
    windows = jnp.dot(shifted, window_table(), precision=lax.Precision.HIGHEST).reshape(
        n_tm, chunk, 2, FS
    )
    windows = jnp.broadcast_to(
        windows[:, None], (n_tm, n_sub, chunk, 2, FS)
    ).reshape(devices, chunk, 2, FS)
    gathered = lax.all_to_all(
        windows, ("tm", "sub"), split_axis=0, concat_axis=0, tiled=True
    ).reshape(SG, 2, FS)

    facet = lax.axis_index("tm")
    band = lax.axis_index("sub")
    first_y = offsets[facet, 0] + band * facet_rows
    ys = first_y + jnp.arange(facet_rows, dtype=jnp.int32)
    order = jnp.arange(SG, dtype=jnp.int32)
    rs = (
        ((order // half_chunk) % 2) * (SG // 2)
        + (order // chunk) * half_chunk
        + order % half_chunk
    )
    angle = ((ys[:, None] * rs[None, :]) % SG).astype(jnp.float32) * (2.0 * math.pi / SG)
    scale = 1.0 / math.sqrt(SG)
    left = jnp.concatenate([jnp.cos(angle) * scale, jnp.sin(angle) * scale], 1)
    real_part = gathered[:, 0]
    imag_part = gathered[:, 1]
    right = jnp.concatenate(
        [
            jnp.concatenate([real_part, imag_part], 1),
            jnp.concatenate([imag_part, -real_part], 1),
        ],
        0,
    )
    summed = jnp.dot(left, right, precision=lax.Precision.HIGHEST).reshape(
        1, facet_rows, 2, FS
    )
    return summed * correction[:, :, None, :]


def solution(mesh):
    in_specs = (
        P(("tm", "sub"), None, None),
        P(("tm", "sub"), None, None),
        P(("tm", "sub"), None),
        P(("tm", "sub")),
        P(("tm", "sub")),
        P(("tm", "sub")),
        P(),
        P("tm", "sub", None),
    )
    out_specs = P("tm", "sub", None, None)
    return jax.shard_map(body, mesh=mesh, in_specs=in_specs, out_specs=out_specs, check_vma=False)
```

```python
import math

import jax
import jax.numpy as jnp
from jax import lax
from jax.experimental import pallas as pl
from jax.experimental.pallas import tpu as pltpu
from jax.sharding import PartitionSpec as P

SG = 512
PATCH = 32
FS = 128
VIS = 1024
SG_PER = 16


kernel_width = 0.7
gauss_scale = -0.5 / (kernel_width * kernel_width) / math.log(2.0)


def split_bf16(x):
    high = x.astype(jnp.bfloat16)
    low = (x - high.astype(jnp.float32)).astype(jnp.bfloat16)
    return jnp.concatenate([high, low], axis=0)


def patch_kernel(place_ref, coords_ref, values_ref, phase_ref, out_ref):
    step = coords_ref.shape[0]
    width = 2 * PATCH
    cells = lax.broadcasted_iota(jnp.int32, (PATCH, 1), 0).astype(jnp.float32)
    lane_half = lax.broadcasted_iota(jnp.int32, (PATCH, 2 * width), 1) // width

    @pl.when(pl.program_id(0) == 0)
    def _():
        out_ref[...] = jnp.zeros_like(out_ref)

    def one_block(i, carry):
        x = coords_ref[i, 0:1, :]
        y = coords_ref[i, 1:2, :]
        rows_kernel = jnp.exp2(((x - cells) ** 2) * gauss_scale)
        cols_kernel = jnp.exp2(((y - cells) ** 2) * gauss_scale)
        weighted = jnp.concatenate(
            [cols_kernel * values_ref[i, 0:1, :], cols_kernel * values_ref[i, 1:2, :]], axis=0
        )
        both = lax.dot_general(
            split_bf16(rows_kernel),
            split_bf16(weighted),
            (((1,), (1,)), ((), ())),
            preferred_element_type=jnp.float32,
        )
        both = both + pltpu.roll(both, width, 1)
        plain = both[:PATCH] + both[PATCH:]
        swapped = pltpu.roll(plain, PATCH, 1)
        phase = phase_ref[pl.ds(i, 1), :]
        phased = plain * phase[:, : 2 * width] + swapped * phase[:, 2 * width :]
        tile = place_ref[pl.program_id(0) * step + i]
        row_tile = tile // (SG // PATCH)
        col_tile = tile % (SG // PATCH)
        rows = pl.ds(pl.multiple_of(row_tile * PATCH, PATCH), PATCH)
        start = pl.multiple_of((col_tile // 2) * 2 * width, 2 * width)
        out_ref[rows, pl.ds(start, 2 * width)] += jnp.where(
            lane_half == col_tile % 2, phased, 0.0
        )
        return carry

    lax.fori_loop(0, step, one_block, 0, unroll=8)


def make_phased_grid(vis_coords, vis_values, live, local, tile_id):
    count = vis_coords.shape[0]
    step = 8
    phase = (jnp.arange(PATCH, dtype=jnp.int32)[None, :] * local[:, None]) % SG_PER
    angle = phase.astype(jnp.float32) * (2.0 * math.pi / SG_PER)
    keep = live.astype(jnp.float32)[:, None]
    cos_b = jnp.cos(angle) * keep
    sin_b = jnp.sin(angle) * keep
    phases = jnp.concatenate(
        [cos_b, cos_b, cos_b, cos_b, sin_b, -sin_b, sin_b, -sin_b], axis=1
    )
    spec = pl.BlockSpec((step, 2, VIS), lambda i, place: (i, 0, 0))
    return pl.pallas_call(
        patch_kernel,
        grid_spec=pltpu.PrefetchScalarGridSpec(
            num_scalar_prefetch=1,
            grid=(count // step,),
            in_specs=[
                spec,
                spec,
                pl.BlockSpec((step, 8 * PATCH), lambda i, place: (i, 0)),
            ],
            out_specs=pl.BlockSpec((SG, 2 * SG), lambda i, place: (0, 0)),
        ),
        out_shape=jax.ShapeDtypeStruct((SG, 2 * SG), jnp.float32),
        cost_estimate=pl.CostEstimate(
            flops=count * 4 * PATCH * 4 * PATCH * VIS * 2,
            transcendentals=count * 2 * PATCH * VIS,
            bytes_accessed=count * 4 * VIS * 4 + SG * SG * 8,
        ),
    )(tile_id, vis_coords, vis_values, phases)


def window_table():
    cs = jnp.arange(SG, dtype=jnp.int32)
    xs = jnp.arange(FS, dtype=jnp.int32)
    angle = ((cs[:, None] * xs[None, :]) % SG).astype(jnp.float32) * (2.0 * math.pi / SG)
    scale = 1.0 / math.sqrt(SG)
    cosine = jnp.cos(angle) * scale
    sine = jnp.sin(angle) * scale
    return jnp.concatenate(
        [jnp.concatenate([cosine, -sine], 1), jnp.concatenate([sine, cosine], 1)], 0
    )


def body(
    vis_coords,
    vis_values,
    block_dest,
    block_local,
    block_tile,
    block_counts,
    facet_offsets,
    correction,
):
    n_tm = lax.axis_size("tm")
    n_sub = lax.axis_size("sub")
    devices = n_tm * n_sub
    blocks = vis_coords.shape[0]
    band_rows = SG // n_sub
    band_tiles = band_rows // PATCH
    col_tiles = SG // PATCH
    tiles_all = col_tiles * col_tiles
    chunk = SG // devices
    facet_rows = FS // n_sub

    live = jnp.arange(blocks, dtype=jnp.int32) < block_counts[0]
    target = block_dest[:, 0]
    row_tile = (target % n_sub) * band_tiles + block_tile // col_tiles
    core = lax.axis_index("tm") % 2
    row_tile = (row_tile + core * (col_tiles // 2)) % col_tiles
    tile_id = row_tile * col_tiles + block_tile % col_tiles
    grid = make_phased_grid(vis_coords, vis_values, live, block_local, tile_id)

    pair = [(i, i ^ 1) for i in range(n_tm)]
    chip_half = grid[: SG // 2] + lax.ppermute(grid[SG // 2 :], "tm", pair)
    half_chunk = chunk // 2
    arrived = lax.all_to_all(
        chip_half.reshape(devices, half_chunk, 2, SG),
        ("tm", "sub"),
        split_axis=0,
        concat_axis=0,
        tiled=True,
    )
    grid_rows = jnp.sum(
        arrived.reshape(n_tm // 2, 2, n_sub, half_chunk, 2, SG), axis=(0, 2)
    )
    grid_rows = (
        grid_rows.reshape(chunk, col_tiles, 2, PATCH).transpose(0, 2, 1, 3).reshape(chunk, 2 * SG)
    )
    offsets = jnp.clip(facet_offsets, 0, SG - FS)
    cs = jnp.arange(SG, dtype=jnp.int32)
    shift = ((offsets[:, 1][:, None] * cs[None, :]) % SG).astype(jnp.float32) * (
        2.0 * math.pi / SG
    )
    cos_s = jnp.cos(shift)[:, None, :]
    sin_s = jnp.sin(shift)[:, None, :]
    g_re = grid_rows[None, :, :SG]
    g_im = grid_rows[None, :, SG:]
    shifted = jnp.concatenate(
        [g_re * cos_s + g_im * sin_s, g_im * cos_s - g_re * sin_s], axis=2
    ).reshape(n_tm * chunk, 2 * SG)
    windows = jnp.dot(shifted, window_table(), precision=lax.Precision.HIGHEST).reshape(
        n_tm, chunk, 2, FS
    )
    windows = jnp.broadcast_to(
        windows[:, None], (n_tm, n_sub, chunk, 2, FS)
    ).reshape(devices, chunk, 2, FS)
    gathered = lax.all_to_all(
        windows, ("tm", "sub"), split_axis=0, concat_axis=0, tiled=True
    ).reshape(SG, 2, FS)

    facet = lax.axis_index("tm")
    band = lax.axis_index("sub")
    first_y = offsets[facet, 0] + band * facet_rows
    ys = first_y + jnp.arange(facet_rows, dtype=jnp.int32)
    order = jnp.arange(SG, dtype=jnp.int32)
    rs = (
        ((order // half_chunk) % 2) * (SG // 2)
        + (order // chunk) * half_chunk
        + order % half_chunk
    )
    angle = ((ys[:, None] * rs[None, :]) % SG).astype(jnp.float32) * (2.0 * math.pi / SG)
    scale = 1.0 / math.sqrt(SG)
    left = jnp.concatenate([jnp.cos(angle) * scale, jnp.sin(angle) * scale], 1)
    real_part = gathered[:, 0]
    imag_part = gathered[:, 1]
    right = jnp.concatenate(
        [
            jnp.concatenate([real_part, imag_part], 1),
            jnp.concatenate([imag_part, -real_part], 1),
        ],
        0,
    )
    summed = jnp.dot(left, right, precision=lax.Precision.HIGHEST).reshape(
        1, facet_rows, 2, FS
    )
    return summed * correction[:, :, None, :]


def solution(mesh):
    in_specs = (
        P(("tm", "sub"), None, None),
        P(("tm", "sub"), None, None),
        P(("tm", "sub"), None),
        P(("tm", "sub")),
        P(("tm", "sub")),
        P(("tm", "sub")),
        P(),
        P("tm", "sub", None),
    )
    out_specs = P("tm", "sub", None, None)
    return jax.shard_map(body, mesh=mesh, in_specs=in_specs, out_specs=out_specs, check_vma=False)
```

```python
import math

import jax
import jax.numpy as jnp
from jax import lax
from jax.experimental import pallas as pl
from jax.experimental.pallas import tpu as pltpu
from jax.sharding import PartitionSpec as P

SG = 512
PATCH = 32
FS = 128
VIS = 1024
SG_PER = 16


kernel_width = 0.7
gauss_scale = -0.5 / (kernel_width * kernel_width) / math.log(2.0)


def split_bf16(x):
    high = x.astype(jnp.bfloat16)
    low = (x - high.astype(jnp.float32)).astype(jnp.bfloat16)
    return jnp.concatenate([high, low], axis=0)


def patch_kernel(place_ref, coords_ref, values_ref, phase_ref, out_ref):
    step = coords_ref.shape[0]
    width = 2 * PATCH
    cells = lax.broadcasted_iota(jnp.int32, (PATCH, 1), 0).astype(jnp.float32)
    lane_half = lax.broadcasted_iota(jnp.int32, (PATCH, 2 * width), 1) // width

    @pl.when(pl.program_id(0) == 0)
    def _():
        out_ref[...] = jnp.zeros_like(out_ref)

    def one_block(i, carry):
        x = coords_ref[i, 0:1, :]
        y = coords_ref[i, 1:2, :]
        rows_kernel = jnp.exp2(((x - cells) ** 2) * gauss_scale)
        cols_kernel = jnp.exp2(((y - cells) ** 2) * gauss_scale)
        weighted = jnp.concatenate(
            [cols_kernel * values_ref[i, 0:1, :], cols_kernel * values_ref[i, 1:2, :]], axis=0
        )
        both = lax.dot_general(
            split_bf16(rows_kernel),
            split_bf16(weighted),
            (((1,), (1,)), ((), ())),
            preferred_element_type=jnp.float32,
        )
        both = both + pltpu.roll(both, width, 1)
        plain = both[:PATCH] + both[PATCH:]
        swapped = pltpu.roll(plain, PATCH, 1)
        phase = phase_ref[pl.ds(i, 1), :]
        phased = plain * phase[:, : 2 * width] + swapped * phase[:, 2 * width :]
        tile = place_ref[pl.program_id(0) * step + i]
        row_tile = tile // (SG // PATCH)
        col_tile = tile % (SG // PATCH)
        rows = pl.ds(pl.multiple_of(row_tile * PATCH, PATCH), PATCH)
        start = pl.multiple_of((col_tile // 2) * 2 * width, 2 * width)
        out_ref[rows, pl.ds(start, 2 * width)] += jnp.where(
            lane_half == col_tile % 2, phased, 0.0
        )
        return carry

    lax.fori_loop(0, step, one_block, 0, unroll=8)


def make_phased_grid(vis_coords, vis_values, live, local, tile_id):
    count = vis_coords.shape[0]
    step = 8
    phase = (jnp.arange(PATCH, dtype=jnp.int32)[None, :] * local[:, None]) % SG_PER
    angle = phase.astype(jnp.float32) * (2.0 * math.pi / SG_PER)
    keep = live.astype(jnp.float32)[:, None]
    cos_b = jnp.cos(angle) * keep
    sin_b = jnp.sin(angle) * keep
    phases = jnp.concatenate(
        [cos_b, cos_b, cos_b, cos_b, sin_b, -sin_b, sin_b, -sin_b], axis=1
    )
    spec = pl.BlockSpec((step, 2, VIS), lambda i, place: (i, 0, 0))
    return pl.pallas_call(
        patch_kernel,
        grid_spec=pltpu.PrefetchScalarGridSpec(
            num_scalar_prefetch=1,
            grid=(count // step,),
            in_specs=[
                spec,
                spec,
                pl.BlockSpec((step, 8 * PATCH), lambda i, place: (i, 0)),
            ],
            out_specs=pl.BlockSpec((SG, 2 * SG), lambda i, place: (0, 0)),
        ),
        out_shape=jax.ShapeDtypeStruct((SG, 2 * SG), jnp.float32),
        cost_estimate=pl.CostEstimate(
            flops=count * 4 * PATCH * 4 * PATCH * VIS * 2,
            transcendentals=count * 2 * PATCH * VIS,
            bytes_accessed=count * 4 * VIS * 4 + SG * SG * 8,
        ),
    )(tile_id, vis_coords, vis_values, phases)


def window_table():
    cs = jnp.arange(SG, dtype=jnp.int32)
    xs = jnp.arange(FS, dtype=jnp.int32)
    angle = ((cs[:, None] * xs[None, :]) % SG).astype(jnp.float32) * (2.0 * math.pi / SG)
    scale = 1.0 / math.sqrt(SG)
    cosine = jnp.cos(angle) * scale
    sine = jnp.sin(angle) * scale
    return jnp.concatenate(
        [jnp.concatenate([cosine, -sine], 1), jnp.concatenate([sine, cosine], 1)], 0
    )


def body(
    vis_coords,
    vis_values,
    block_dest,
    block_local,
    block_tile,
    block_counts,
    facet_offsets,
    correction,
):
    n_tm = lax.axis_size("tm")
    n_sub = lax.axis_size("sub")
    devices = n_tm * n_sub
    blocks = vis_coords.shape[0]
    band_rows = SG // n_sub
    band_tiles = band_rows // PATCH
    col_tiles = SG // PATCH
    tiles_all = col_tiles * col_tiles
    chunk = SG // devices
    facet_rows = FS // n_sub

    live = jnp.arange(blocks, dtype=jnp.int32) < block_counts[0]
    target = block_dest[:, 0]
    row_tile = (target % n_sub) * band_tiles + block_tile // col_tiles
    core = lax.axis_index("tm") % 2
    row_tile = (row_tile + core * (col_tiles // 2)) % col_tiles
    tile_id = row_tile * col_tiles + block_tile % col_tiles
    grid = make_phased_grid(vis_coords, vis_values, live, block_local, tile_id)

    pair = [(i, i ^ 1) for i in range(n_tm)]
    chip_half = grid[: SG // 2] + lax.ppermute(grid[SG // 2 :], "tm", pair)
    half_chunk = chunk // 2
    arrived = lax.all_to_all(
        chip_half.reshape(devices, half_chunk, 2, SG),
        ("tm", "sub"),
        split_axis=0,
        concat_axis=0,
        tiled=True,
    )
    grid_rows = jnp.sum(
        arrived.reshape(n_tm // 2, 2, n_sub, half_chunk, 2, SG), axis=(0, 2)
    )
    grid_rows = (
        grid_rows.reshape(chunk, col_tiles, 2, PATCH).transpose(0, 2, 1, 3).reshape(chunk, 2 * SG)
    )
    offsets = jnp.clip(facet_offsets, 0, SG - FS)
    cs = jnp.arange(SG, dtype=jnp.int32)
    shift = ((offsets[:, 1][:, None] * cs[None, :]) % SG).astype(jnp.float32) * (
        2.0 * math.pi / SG
    )
    cos_s = jnp.cos(shift)[:, None, :]
    sin_s = jnp.sin(shift)[:, None, :]
    g_re = grid_rows[None, :, :SG]
    g_im = grid_rows[None, :, SG:]
    shifted = jnp.concatenate(
        [g_re * cos_s + g_im * sin_s, g_im * cos_s - g_re * sin_s], axis=2
    ).reshape(n_tm * chunk, 2 * SG)
    windows = jnp.dot(shifted, window_table(), precision=lax.Precision.HIGHEST).reshape(
        n_tm, chunk, 2, FS
    )
    gathered = lax.all_to_all(windows, "tm", split_axis=0, concat_axis=0, tiled=True)
    gathered = gathered.reshape(n_tm * chunk, 2, FS)

    facet = lax.axis_index("tm")
    band = lax.axis_index("sub")
    ys = offsets[facet, 0] + jnp.arange(FS, dtype=jnp.int32)
    order = jnp.arange(n_tm * chunk, dtype=jnp.int32)
    rs = (
        ((order // half_chunk) % 2) * (SG // 2)
        + ((order // chunk) * n_sub + band) * half_chunk
        + order % half_chunk
    )
    angle = ((ys[:, None] * rs[None, :]) % SG).astype(jnp.float32) * (2.0 * math.pi / SG)
    scale = 1.0 / math.sqrt(SG)
    left = jnp.concatenate([jnp.cos(angle) * scale, jnp.sin(angle) * scale], 1)
    real_part = gathered[:, 0]
    imag_part = gathered[:, 1]
    right = jnp.concatenate(
        [
            jnp.concatenate([real_part, imag_part], 1),
            jnp.concatenate([imag_part, -real_part], 1),
        ],
        0,
    )
    partial = jnp.dot(left, right, precision=lax.Precision.HIGHEST).reshape(
        n_sub, facet_rows, 2, FS
    )
    summed = jnp.sum(
        lax.all_to_all(partial, "sub", split_axis=0, concat_axis=0, tiled=True)
        .reshape(n_sub, facet_rows, 2, FS),
        axis=0,
    )[None]
    return summed * correction[:, :, None, :]


def solution(mesh):
    in_specs = (
        P(("tm", "sub"), None, None),
        P(("tm", "sub"), None, None),
        P(("tm", "sub"), None),
        P(("tm", "sub")),
        P(("tm", "sub")),
        P(("tm", "sub")),
        P(),
        P("tm", "sub", None),
    )
    out_specs = P("tm", "sub", None, None)
    return jax.shard_map(body, mesh=mesh, in_specs=in_specs, out_specs=out_specs, check_vma=False)
```

```python
import math

import jax
import jax.numpy as jnp
from jax import lax
from jax.experimental import pallas as pl
from jax.experimental.pallas import tpu as pltpu
from jax.sharding import PartitionSpec as P

SG = 512
PATCH = 32
FS = 128
VIS = 1024
SG_PER = 16


kernel_width = 0.7
gauss_scale = -0.5 / (kernel_width * kernel_width) / math.log(2.0)


def split_bf16(x):
    high = x.astype(jnp.bfloat16)
    low = (x - high.astype(jnp.float32)).astype(jnp.bfloat16)
    return jnp.concatenate([high, low], axis=0)


def patch_kernel(place_ref, coords_ref, values_ref, phase_ref, out_ref):
    step = coords_ref.shape[0]
    width = 2 * PATCH
    cells = lax.broadcasted_iota(jnp.int32, (PATCH, 1), 0).astype(jnp.float32)
    lane_half = lax.broadcasted_iota(jnp.int32, (PATCH, 2 * width), 1) // width

    @pl.when(pl.program_id(0) == 0)
    def _():
        out_ref[...] = jnp.zeros_like(out_ref)

    def one_block(i, carry):
        x = coords_ref[i, 0:1, :]
        y = coords_ref[i, 1:2, :]
        rows_kernel = jnp.exp2(((x - cells) ** 2) * gauss_scale)
        cols_kernel = jnp.exp2(((y - cells) ** 2) * gauss_scale)
        weighted = jnp.concatenate(
            [cols_kernel * values_ref[i, 0:1, :], cols_kernel * values_ref[i, 1:2, :]], axis=0
        )
        both = lax.dot_general(
            split_bf16(rows_kernel),
            split_bf16(weighted),
            (((1,), (1,)), ((), ())),
            preferred_element_type=jnp.float32,
        )
        both = both + pltpu.roll(both, width, 1)
        plain = both[:PATCH] + both[PATCH:]
        swapped = pltpu.roll(plain, PATCH, 1)
        phase = phase_ref[pl.ds(i, 1), :]
        phased = plain * phase[:, : 2 * width] + swapped * phase[:, 2 * width :]
        tile = place_ref[pl.program_id(0) * step + i]
        row_tile = tile // (SG // PATCH)
        col_tile = tile % (SG // PATCH)
        rows = pl.ds(pl.multiple_of(row_tile * PATCH, PATCH), PATCH)
        start = pl.multiple_of((col_tile // 2) * 2 * width, 2 * width)
        out_ref[rows, pl.ds(start, 2 * width)] += jnp.where(
            lane_half == col_tile % 2, phased, 0.0
        )
        return carry

    lax.fori_loop(0, step, one_block, 0, unroll=16)


def make_phased_grid(vis_coords, vis_values, live, local, tile_id):
    count = vis_coords.shape[0]
    step = 16
    phase = (jnp.arange(PATCH, dtype=jnp.int32)[None, :] * local[:, None]) % SG_PER
    angle = phase.astype(jnp.float32) * (2.0 * math.pi / SG_PER)
    keep = live.astype(jnp.float32)[:, None]
    cos_b = jnp.cos(angle) * keep
    sin_b = jnp.sin(angle) * keep
    phases = jnp.concatenate(
        [cos_b, cos_b, cos_b, cos_b, sin_b, -sin_b, sin_b, -sin_b], axis=1
    )
    spec = pl.BlockSpec((step, 2, VIS), lambda i, place: (i, 0, 0))
    return pl.pallas_call(
        patch_kernel,
        grid_spec=pltpu.PrefetchScalarGridSpec(
            num_scalar_prefetch=1,
            grid=(count // step,),
            in_specs=[
                spec,
                spec,
                pl.BlockSpec((step, 8 * PATCH), lambda i, place: (i, 0)),
            ],
            out_specs=pl.BlockSpec((SG, 2 * SG), lambda i, place: (0, 0)),
        ),
        out_shape=jax.ShapeDtypeStruct((SG, 2 * SG), jnp.float32),
        cost_estimate=pl.CostEstimate(
            flops=count * 4 * PATCH * 4 * PATCH * VIS * 2,
            transcendentals=count * 2 * PATCH * VIS,
            bytes_accessed=count * 4 * VIS * 4 + SG * SG * 8,
        ),
    )(tile_id, vis_coords, vis_values, phases)


def window_table():
    cs = jnp.arange(SG, dtype=jnp.int32)
    xs = jnp.arange(FS, dtype=jnp.int32)
    angle = ((cs[:, None] * xs[None, :]) % SG).astype(jnp.float32) * (2.0 * math.pi / SG)
    scale = 1.0 / math.sqrt(SG)
    cosine = jnp.cos(angle) * scale
    sine = jnp.sin(angle) * scale
    return jnp.concatenate(
        [jnp.concatenate([cosine, -sine], 1), jnp.concatenate([sine, cosine], 1)], 0
    )


def body(
    vis_coords,
    vis_values,
    block_dest,
    block_local,
    block_tile,
    block_counts,
    facet_offsets,
    correction,
):
    n_tm = lax.axis_size("tm")
    n_sub = lax.axis_size("sub")
    devices = n_tm * n_sub
    blocks = vis_coords.shape[0]
    band_rows = SG // n_sub
    band_tiles = band_rows // PATCH
    col_tiles = SG // PATCH
    tiles_all = col_tiles * col_tiles
    chunk = SG // devices
    facet_rows = FS // n_sub

    live = jnp.arange(blocks, dtype=jnp.int32) < block_counts[0]
    target = block_dest[:, 0]
    row_tile = (target % n_sub) * band_tiles + block_tile // col_tiles
    core = lax.axis_index("tm") % 2
    row_tile = (row_tile + core * (col_tiles // 2)) % col_tiles
    tile_id = row_tile * col_tiles + block_tile % col_tiles
    grid = make_phased_grid(vis_coords, vis_values, live, block_local, tile_id)

    pair = [(i, i ^ 1) for i in range(n_tm)]
    chip_half = grid[: SG // 2] + lax.ppermute(grid[SG // 2 :], "tm", pair)
    half_chunk = chunk // 2
    arrived = lax.all_to_all(
        chip_half.reshape(devices, half_chunk, 2, SG),
        ("tm", "sub"),
        split_axis=0,
        concat_axis=0,
        tiled=True,
    )
    grid_rows = jnp.sum(
        arrived.reshape(n_tm // 2, 2, n_sub, half_chunk, 2, SG), axis=(0, 2)
    )
    grid_rows = (
        grid_rows.reshape(chunk, col_tiles, 2, PATCH).transpose(0, 2, 1, 3).reshape(chunk, 2 * SG)
    )
    offsets = jnp.clip(facet_offsets, 0, SG - FS)
    cs = jnp.arange(SG, dtype=jnp.int32)
    shift = ((offsets[:, 1][:, None] * cs[None, :]) % SG).astype(jnp.float32) * (
        2.0 * math.pi / SG
    )
    cos_s = jnp.cos(shift)[:, None, :]
    sin_s = jnp.sin(shift)[:, None, :]
    g_re = grid_rows[None, :, :SG]
    g_im = grid_rows[None, :, SG:]
    shifted = jnp.concatenate(
        [g_re * cos_s + g_im * sin_s, g_im * cos_s - g_re * sin_s], axis=2
    ).reshape(n_tm * chunk, 2 * SG)
    windows = jnp.dot(shifted, window_table(), precision=lax.Precision.HIGHEST).reshape(
        n_tm, chunk, 2, FS
    )
    windows = jnp.broadcast_to(
        windows[:, None], (n_tm, n_sub, chunk, 2, FS)
    ).reshape(devices, chunk, 2, FS)
    gathered = lax.all_to_all(
        windows, ("tm", "sub"), split_axis=0, concat_axis=0, tiled=True
    ).reshape(SG, 2, FS)

    facet = lax.axis_index("tm")
    band = lax.axis_index("sub")
    first_y = offsets[facet, 0] + band * facet_rows
    ys = first_y + jnp.arange(facet_rows, dtype=jnp.int32)
    order = jnp.arange(SG, dtype=jnp.int32)
    rs = (
        ((order // half_chunk) % 2) * (SG // 2)
        + (order // chunk) * half_chunk
        + order % half_chunk
    )
    angle = ((ys[:, None] * rs[None, :]) % SG).astype(jnp.float32) * (2.0 * math.pi / SG)
    scale = 1.0 / math.sqrt(SG)
    left = jnp.concatenate([jnp.cos(angle) * scale, jnp.sin(angle) * scale], 1)
    real_part = gathered[:, 0]
    imag_part = gathered[:, 1]
    right = jnp.concatenate(
        [
            jnp.concatenate([real_part, imag_part], 1),
            jnp.concatenate([imag_part, -real_part], 1),
        ],
        0,
    )
    summed = jnp.dot(left, right, precision=lax.Precision.HIGHEST).reshape(
        1, facet_rows, 2, FS
    )
    return summed * correction[:, :, None, :]


def solution(mesh):
    in_specs = (
        P(("tm", "sub"), None, None),
        P(("tm", "sub"), None, None),
        P(("tm", "sub"), None),
        P(("tm", "sub")),
        P(("tm", "sub")),
        P(("tm", "sub")),
        P(),
        P("tm", "sub", None),
    )
    out_specs = P("tm", "sub", None, None)
    return jax.shard_map(body, mesh=mesh, in_specs=in_specs, out_specs=out_specs, check_vma=False)
```

```python
import math

import jax
import jax.numpy as jnp
from jax import lax
from jax.experimental import pallas as pl
from jax.experimental.pallas import tpu as pltpu
from jax.sharding import PartitionSpec as P

SG = 512
PATCH = 32
FS = 128
VIS = 1024
SG_PER = 16


kernel_width = 0.7
gauss_scale = -0.5 / (kernel_width * kernel_width) / math.log(2.0)


def split_bf16(x):
    high = x.astype(jnp.bfloat16)
    low = (x - high.astype(jnp.float32)).astype(jnp.bfloat16)
    return jnp.concatenate([high, low], axis=0)


def patch_kernel(place_ref, coords_ref, values_ref, phase_ref, out_ref):
    step = coords_ref.shape[0]
    width = 2 * PATCH
    cells = lax.broadcasted_iota(jnp.int32, (PATCH, 1), 0).astype(jnp.float32)
    lane_half = lax.broadcasted_iota(jnp.int32, (PATCH, 2 * width), 1) // width

    @pl.when(pl.program_id(0) == 0)
    def _():
        out_ref[...] = jnp.zeros_like(out_ref)

    def one_block(i, carry):
        x = coords_ref[i, 0:1, :]
        y = coords_ref[i, 1:2, :]
        rows_kernel = jnp.exp2(((x - cells) ** 2) * gauss_scale)
        cols_kernel = jnp.exp2(((y - cells) ** 2) * gauss_scale)
        weighted = jnp.concatenate(
            [cols_kernel * values_ref[i, 0:1, :], cols_kernel * values_ref[i, 1:2, :]], axis=0
        )
        both = lax.dot_general(
            split_bf16(rows_kernel),
            split_bf16(weighted),
            (((1,), (1,)), ((), ())),
            preferred_element_type=jnp.float32,
        )
        both = both + pltpu.roll(both, width, 1)
        plain = both[:PATCH] + both[PATCH:]
        swapped = pltpu.roll(plain, PATCH, 1)
        phase = phase_ref[pl.ds(i, 1), :]
        phased = plain * phase[:, : 2 * width] + swapped * phase[:, 2 * width :]
        tile = place_ref[pl.program_id(0) * step + i]
        row_tile = tile // (SG // PATCH)
        col_tile = tile % (SG // PATCH)
        rows = pl.ds(pl.multiple_of(row_tile * PATCH, PATCH), PATCH)
        start = pl.multiple_of((col_tile // 2) * 2 * width, 2 * width)
        out_ref[rows, pl.ds(start, 2 * width)] += jnp.where(
            lane_half == col_tile % 2, phased, 0.0
        )
        return carry

    lax.fori_loop(0, step, one_block, 0, unroll=32)


def make_phased_grid(vis_coords, vis_values, live, local, tile_id):
    count = vis_coords.shape[0]
    step = 32
    phase = (jnp.arange(PATCH, dtype=jnp.int32)[None, :] * local[:, None]) % SG_PER
    angle = phase.astype(jnp.float32) * (2.0 * math.pi / SG_PER)
    keep = live.astype(jnp.float32)[:, None]
    cos_b = jnp.cos(angle) * keep
    sin_b = jnp.sin(angle) * keep
    phases = jnp.concatenate(
        [cos_b, cos_b, cos_b, cos_b, sin_b, -sin_b, sin_b, -sin_b], axis=1
    )
    spec = pl.BlockSpec((step, 2, VIS), lambda i, place: (i, 0, 0))
    return pl.pallas_call(
        patch_kernel,
        grid_spec=pltpu.PrefetchScalarGridSpec(
            num_scalar_prefetch=1,
            grid=(count // step,),
            in_specs=[
                spec,
                spec,
                pl.BlockSpec((step, 8 * PATCH), lambda i, place: (i, 0)),
            ],
            out_specs=pl.BlockSpec((SG, 2 * SG), lambda i, place: (0, 0)),
        ),
        out_shape=jax.ShapeDtypeStruct((SG, 2 * SG), jnp.float32),
        cost_estimate=pl.CostEstimate(
            flops=count * 4 * PATCH * 4 * PATCH * VIS * 2,
            transcendentals=count * 2 * PATCH * VIS,
            bytes_accessed=count * 4 * VIS * 4 + SG * SG * 8,
        ),
    )(tile_id, vis_coords, vis_values, phases)


def window_table():
    cs = jnp.arange(SG, dtype=jnp.int32)
    xs = jnp.arange(FS, dtype=jnp.int32)
    angle = ((cs[:, None] * xs[None, :]) % SG).astype(jnp.float32) * (2.0 * math.pi / SG)
    scale = 1.0 / math.sqrt(SG)
    cosine = jnp.cos(angle) * scale
    sine = jnp.sin(angle) * scale
    return jnp.concatenate(
        [jnp.concatenate([cosine, -sine], 1), jnp.concatenate([sine, cosine], 1)], 0
    )


def body(
    vis_coords,
    vis_values,
    block_dest,
    block_local,
    block_tile,
    block_counts,
    facet_offsets,
    correction,
):
    n_tm = lax.axis_size("tm")
    n_sub = lax.axis_size("sub")
    devices = n_tm * n_sub
    blocks = vis_coords.shape[0]
    band_rows = SG // n_sub
    band_tiles = band_rows // PATCH
    col_tiles = SG // PATCH
    tiles_all = col_tiles * col_tiles
    chunk = SG // devices
    facet_rows = FS // n_sub

    live = jnp.arange(blocks, dtype=jnp.int32) < block_counts[0]
    target = block_dest[:, 0]
    row_tile = (target % n_sub) * band_tiles + block_tile // col_tiles
    core = lax.axis_index("tm") % 2
    row_tile = (row_tile + core * (col_tiles // 2)) % col_tiles
    tile_id = row_tile * col_tiles + block_tile % col_tiles
    grid = make_phased_grid(vis_coords, vis_values, live, block_local, tile_id)

    pair = [(i, i ^ 1) for i in range(n_tm)]
    chip_half = grid[: SG // 2] + lax.ppermute(grid[SG // 2 :], "tm", pair)
    half_chunk = chunk // 2
    arrived = lax.all_to_all(
        chip_half.reshape(devices, half_chunk, 2, SG),
        ("tm", "sub"),
        split_axis=0,
        concat_axis=0,
        tiled=True,
    )
    grid_rows = jnp.sum(
        arrived.reshape(n_tm // 2, 2, n_sub, half_chunk, 2, SG), axis=(0, 2)
    )
    grid_rows = (
        grid_rows.reshape(chunk, col_tiles, 2, PATCH).transpose(0, 2, 1, 3).reshape(chunk, 2 * SG)
    )
    offsets = jnp.clip(facet_offsets, 0, SG - FS)
    cs = jnp.arange(SG, dtype=jnp.int32)
    shift = ((offsets[:, 1][:, None] * cs[None, :]) % SG).astype(jnp.float32) * (
        2.0 * math.pi / SG
    )
    cos_s = jnp.cos(shift)[:, None, :]
    sin_s = jnp.sin(shift)[:, None, :]
    g_re = grid_rows[None, :, :SG]
    g_im = grid_rows[None, :, SG:]
    shifted = jnp.concatenate(
        [g_re * cos_s + g_im * sin_s, g_im * cos_s - g_re * sin_s], axis=2
    ).reshape(n_tm * chunk, 2 * SG)
    windows = jnp.dot(shifted, window_table(), precision=lax.Precision.HIGHEST).reshape(
        n_tm, chunk, 2, FS
    )
    windows = jnp.broadcast_to(
        windows[:, None], (n_tm, n_sub, chunk, 2, FS)
    ).reshape(devices, chunk, 2, FS)
    gathered = lax.all_to_all(
        windows, ("tm", "sub"), split_axis=0, concat_axis=0, tiled=True
    ).reshape(SG, 2, FS)

    facet = lax.axis_index("tm")
    band = lax.axis_index("sub")
    first_y = offsets[facet, 0] + band * facet_rows
    ys = first_y + jnp.arange(facet_rows, dtype=jnp.int32)
    order = jnp.arange(SG, dtype=jnp.int32)
    rs = (
        ((order // half_chunk) % 2) * (SG // 2)
        + (order // chunk) * half_chunk
        + order % half_chunk
    )
    angle = ((ys[:, None] * rs[None, :]) % SG).astype(jnp.float32) * (2.0 * math.pi / SG)
    scale = 1.0 / math.sqrt(SG)
    left = jnp.concatenate([jnp.cos(angle) * scale, jnp.sin(angle) * scale], 1)
    real_part = gathered[:, 0]
    imag_part = gathered[:, 1]
    right = jnp.concatenate(
        [
            jnp.concatenate([real_part, imag_part], 1),
            jnp.concatenate([imag_part, -real_part], 1),
        ],
        0,
    )
    summed = jnp.dot(left, right, precision=lax.Precision.HIGHEST).reshape(
        1, facet_rows, 2, FS
    )
    return summed * correction[:, :, None, :]


def solution(mesh):
    in_specs = (
        P(("tm", "sub"), None, None),
        P(("tm", "sub"), None, None),
        P(("tm", "sub"), None),
        P(("tm", "sub")),
        P(("tm", "sub")),
        P(("tm", "sub")),
        P(),
        P("tm", "sub", None),
    )
    out_specs = P("tm", "sub", None, None)
    return jax.shard_map(body, mesh=mesh, in_specs=in_specs, out_specs=out_specs, check_vma=False)
```

```python
import math

import jax
import jax.numpy as jnp
from jax import lax
from jax.experimental import pallas as pl
from jax.experimental.pallas import tpu as pltpu
from jax.sharding import PartitionSpec as P

SG = 512
PATCH = 32
FS = 128
VIS = 1024
SG_PER = 16


kernel_width = 0.7
gauss_scale = -0.5 / (kernel_width * kernel_width) / math.log(2.0)


def split_bf16(x):
    high = x.astype(jnp.bfloat16)
    low = (x - high.astype(jnp.float32)).astype(jnp.bfloat16)
    return jnp.concatenate([high, low], axis=0)


def patch_kernel(place_ref, coords_ref, values_ref, phase_ref, out_ref):
    step = coords_ref.shape[0]
    width = 2 * PATCH
    cells = lax.broadcasted_iota(jnp.int32, (PATCH, 1), 0).astype(jnp.float32)
    lane_half = lax.broadcasted_iota(jnp.int32, (PATCH, 2 * width), 1) // width

    @pl.when(pl.program_id(0) == 0)
    def _():
        out_ref[...] = jnp.zeros_like(out_ref)

    def one_block(i, carry):
        x = coords_ref[i, 0:1, :]
        y = coords_ref[i, 1:2, :]
        rows_kernel = jnp.exp2(((x - cells) ** 2) * gauss_scale)
        cols_kernel = jnp.exp2(((y - cells) ** 2) * gauss_scale)
        weighted = jnp.concatenate(
            [cols_kernel * values_ref[i, 0:1, :], cols_kernel * values_ref[i, 1:2, :]], axis=0
        )
        both = lax.dot_general(
            split_bf16(rows_kernel),
            split_bf16(weighted),
            (((1,), (1,)), ((), ())),
            preferred_element_type=jnp.float32,
        )
        both = both + pltpu.roll(both, width, 1)
        plain = both[:PATCH] + both[PATCH:]
        swapped = pltpu.roll(plain, PATCH, 1)
        phase = phase_ref[pl.ds(i, 1), :]
        phased = plain * phase[:, : 2 * width] + swapped * phase[:, 2 * width :]
        tile = place_ref[pl.program_id(0) * step + i]
        row_tile = tile // (SG // PATCH)
        col_tile = tile % (SG // PATCH)
        rows = pl.ds(pl.multiple_of(row_tile * PATCH, PATCH), PATCH)
        start = pl.multiple_of((col_tile // 2) * 2 * width, 2 * width)
        out_ref[rows, pl.ds(start, 2 * width)] += jnp.where(
            lane_half == col_tile % 2, phased, 0.0
        )
        return carry

    lax.fori_loop(0, step, one_block, 0, unroll=64)


def make_phased_grid(vis_coords, vis_values, live, local, tile_id):
    count = vis_coords.shape[0]
    step = 64
    phase = (jnp.arange(PATCH, dtype=jnp.int32)[None, :] * local[:, None]) % SG_PER
    angle = phase.astype(jnp.float32) * (2.0 * math.pi / SG_PER)
    keep = live.astype(jnp.float32)[:, None]
    cos_b = jnp.cos(angle) * keep
    sin_b = jnp.sin(angle) * keep
    phases = jnp.concatenate(
        [cos_b, cos_b, cos_b, cos_b, sin_b, -sin_b, sin_b, -sin_b], axis=1
    )
    spec = pl.BlockSpec((step, 2, VIS), lambda i, place: (i, 0, 0))
    return pl.pallas_call(
        patch_kernel,
        grid_spec=pltpu.PrefetchScalarGridSpec(
            num_scalar_prefetch=1,
            grid=(count // step,),
            in_specs=[
                spec,
                spec,
                pl.BlockSpec((step, 8 * PATCH), lambda i, place: (i, 0)),
            ],
            out_specs=pl.BlockSpec((SG, 2 * SG), lambda i, place: (0, 0)),
        ),
        out_shape=jax.ShapeDtypeStruct((SG, 2 * SG), jnp.float32),
        cost_estimate=pl.CostEstimate(
            flops=count * 4 * PATCH * 4 * PATCH * VIS * 2,
            transcendentals=count * 2 * PATCH * VIS,
            bytes_accessed=count * 4 * VIS * 4 + SG * SG * 8,
        ),
    )(tile_id, vis_coords, vis_values, phases)


def window_table():
    cs = jnp.arange(SG, dtype=jnp.int32)
    xs = jnp.arange(FS, dtype=jnp.int32)
    angle = ((cs[:, None] * xs[None, :]) % SG).astype(jnp.float32) * (2.0 * math.pi / SG)
    scale = 1.0 / math.sqrt(SG)
    cosine = jnp.cos(angle) * scale
    sine = jnp.sin(angle) * scale
    return jnp.concatenate(
        [jnp.concatenate([cosine, -sine], 1), jnp.concatenate([sine, cosine], 1)], 0
    )


def body(
    vis_coords,
    vis_values,
    block_dest,
    block_local,
    block_tile,
    block_counts,
    facet_offsets,
    correction,
):
    n_tm = lax.axis_size("tm")
    n_sub = lax.axis_size("sub")
    devices = n_tm * n_sub
    blocks = vis_coords.shape[0]
    band_rows = SG // n_sub
    band_tiles = band_rows // PATCH
    col_tiles = SG // PATCH
    tiles_all = col_tiles * col_tiles
    chunk = SG // devices
    facet_rows = FS // n_sub

    live = jnp.arange(blocks, dtype=jnp.int32) < block_counts[0]
    target = block_dest[:, 0]
    row_tile = (target % n_sub) * band_tiles + block_tile // col_tiles
    core = lax.axis_index("tm") % 2
    row_tile = (row_tile + core * (col_tiles // 2)) % col_tiles
    tile_id = row_tile * col_tiles + block_tile % col_tiles
    grid = make_phased_grid(vis_coords, vis_values, live, block_local, tile_id)

    pair = [(i, i ^ 1) for i in range(n_tm)]
    chip_half = grid[: SG // 2] + lax.ppermute(grid[SG // 2 :], "tm", pair)
    half_chunk = chunk // 2
    arrived = lax.all_to_all(
        chip_half.reshape(devices, half_chunk, 2, SG),
        ("tm", "sub"),
        split_axis=0,
        concat_axis=0,
        tiled=True,
    )
    grid_rows = jnp.sum(
        arrived.reshape(n_tm // 2, 2, n_sub, half_chunk, 2, SG), axis=(0, 2)
    )
    grid_rows = (
        grid_rows.reshape(chunk, col_tiles, 2, PATCH).transpose(0, 2, 1, 3).reshape(chunk, 2 * SG)
    )
    offsets = jnp.clip(facet_offsets, 0, SG - FS)
    cs = jnp.arange(SG, dtype=jnp.int32)
    shift = ((offsets[:, 1][:, None] * cs[None, :]) % SG).astype(jnp.float32) * (
        2.0 * math.pi / SG
    )
    cos_s = jnp.cos(shift)[:, None, :]
    sin_s = jnp.sin(shift)[:, None, :]
    g_re = grid_rows[None, :, :SG]
    g_im = grid_rows[None, :, SG:]
    shifted = jnp.concatenate(
        [g_re * cos_s + g_im * sin_s, g_im * cos_s - g_re * sin_s], axis=2
    ).reshape(n_tm * chunk, 2 * SG)
    windows = jnp.dot(shifted, window_table(), precision=lax.Precision.HIGHEST).reshape(
        n_tm, chunk, 2, FS
    )
    windows = jnp.broadcast_to(
        windows[:, None], (n_tm, n_sub, chunk, 2, FS)
    ).reshape(devices, chunk, 2, FS)
    gathered = lax.all_to_all(
        windows, ("tm", "sub"), split_axis=0, concat_axis=0, tiled=True
    ).reshape(SG, 2, FS)

    facet = lax.axis_index("tm")
    band = lax.axis_index("sub")
    first_y = offsets[facet, 0] + band * facet_rows
    ys = first_y + jnp.arange(facet_rows, dtype=jnp.int32)
    order = jnp.arange(SG, dtype=jnp.int32)
    rs = (
        ((order // half_chunk) % 2) * (SG // 2)
        + (order // chunk) * half_chunk
        + order % half_chunk
    )
    angle = ((ys[:, None] * rs[None, :]) % SG).astype(jnp.float32) * (2.0 * math.pi / SG)
    scale = 1.0 / math.sqrt(SG)
    left = jnp.concatenate([jnp.cos(angle) * scale, jnp.sin(angle) * scale], 1)
    real_part = gathered[:, 0]
    imag_part = gathered[:, 1]
    right = jnp.concatenate(
        [
            jnp.concatenate([real_part, imag_part], 1),
            jnp.concatenate([imag_part, -real_part], 1),
        ],
        0,
    )
    summed = jnp.dot(left, right, precision=lax.Precision.HIGHEST).reshape(
        1, facet_rows, 2, FS
    )
    return summed * correction[:, :, None, :]


def solution(mesh):
    in_specs = (
        P(("tm", "sub"), None, None),
        P(("tm", "sub"), None, None),
        P(("tm", "sub"), None),
        P(("tm", "sub")),
        P(("tm", "sub")),
        P(("tm", "sub")),
        P(),
        P("tm", "sub", None),
    )
    out_specs = P("tm", "sub", None, None)
    return jax.shard_map(body, mesh=mesh, in_specs=in_specs, out_specs=out_specs, check_vma=False)
```

```python
import functools
import math

import jax
import numpy as np
import jax.numpy as jnp
from jax import lax
from jax.experimental import pallas as pl
from jax.experimental.pallas import tpu as pltpu
from jax.sharding import PartitionSpec as P

SG = 512
PATCH = 32
FS = 128
VIS = 1024
SG_PER = 16


kernel_width = 0.7
gauss_scale = -0.5 / (kernel_width * kernel_width) / math.log(2.0)


def split_bf16(x):
    high = x.astype(jnp.bfloat16)
    low = (x - high.astype(jnp.float32)).astype(jnp.bfloat16)
    return jnp.concatenate([high, low], axis=0)


def patch_kernel(n_sub, dest_ref, tile_ref, local_ref, count_ref, coords_ref, values_ref, phase_ref, out_ref):
    step = coords_ref.shape[0]
    width = 2 * PATCH
    cells = lax.broadcasted_iota(jnp.int32, (PATCH, 1), 0).astype(jnp.float32)
    lane_half = lax.broadcasted_iota(jnp.int32, (PATCH, 2 * width), 1) // width

    @pl.when(pl.program_id(0) == 0)
    def _():
        out_ref[...] = jnp.zeros_like(out_ref)

    def one_block(i, carry):
        x = coords_ref[i, 0:1, :]
        y = coords_ref[i, 1:2, :]
        rows_kernel = jnp.exp2(((x - cells) ** 2) * gauss_scale)
        cols_kernel = jnp.exp2(((y - cells) ** 2) * gauss_scale)
        weighted = jnp.concatenate(
            [cols_kernel * values_ref[i, 0:1, :], cols_kernel * values_ref[i, 1:2, :]], axis=0
        )
        both = lax.dot_general(
            split_bf16(rows_kernel),
            split_bf16(weighted),
            (((1,), (1,)), ((), ())),
            preferred_element_type=jnp.float32,
        )
        both = both + pltpu.roll(both, width, 1)
        plain = both[:PATCH] + both[PATCH:]
        swapped = pltpu.roll(plain, PATCH, 1)
        block = pl.program_id(0) * step + i
        phase = phase_ref[pl.ds(local_ref[block], 1), :]
        phase = jnp.where(block < count_ref[0], phase, 0.0)
        phased = plain * phase[:, : 2 * width] + swapped * phase[:, 2 * width :]
        col_tiles = SG // PATCH
        row_tile = (dest_ref[block] % n_sub) * (col_tiles // n_sub) + tile_ref[block] // col_tiles
        row_tile = (row_tile + (lax.axis_index("tm") % 2) * (col_tiles // 2)) % col_tiles
        col_tile = tile_ref[block] % col_tiles
        rows = pl.ds(pl.multiple_of(row_tile * PATCH, PATCH), PATCH)
        start = pl.multiple_of((col_tile // 2) * 2 * width, 2 * width)
        out_ref[rows, pl.ds(start, 2 * width)] += jnp.where(
            lane_half == col_tile % 2, phased, 0.0
        )
        return carry

    lax.fori_loop(0, step, one_block, 0, unroll=32)


def phase_table():
    b = np.arange(PATCH)
    rows = []
    for local in range(SG_PER):
        angle = ((b * local) % SG_PER) * (2.0 * math.pi / SG_PER)
        cos_b, sin_b = np.cos(angle), np.sin(angle)
        rows.append(np.concatenate([cos_b, cos_b, cos_b, cos_b, sin_b, -sin_b, sin_b, -sin_b]))
    return jnp.asarray(np.stack(rows).astype(np.float32))


def make_phased_grid(n_sub, vis_coords, vis_values, block_dest, block_tile, block_local, block_counts):
    count = vis_coords.shape[0]
    step = 32
    spec = pl.BlockSpec((step, 2, VIS), lambda i, *refs: (i, 0, 0))
    return pl.pallas_call(
        functools.partial(patch_kernel, n_sub),
        grid_spec=pltpu.PrefetchScalarGridSpec(
            num_scalar_prefetch=4,
            grid=(count // step,),
            in_specs=[
                spec,
                spec,
                pl.BlockSpec((SG_PER, 8 * PATCH), lambda i, *refs: (0, 0)),
            ],
            out_specs=pl.BlockSpec((SG, 2 * SG), lambda i, *refs: (0, 0)),
        ),
        out_shape=jax.ShapeDtypeStruct((SG, 2 * SG), jnp.float32),
        cost_estimate=pl.CostEstimate(
            flops=count * 4 * PATCH * 4 * PATCH * VIS * 2,
            transcendentals=count * 2 * PATCH * VIS,
            bytes_accessed=count * 4 * VIS * 4 + SG * SG * 8,
        ),
    )(block_dest[:, 0], block_tile, block_local, block_counts, vis_coords, vis_values, phase_table())


def window_table():
    cs = jnp.arange(SG, dtype=jnp.int32)
    xs = jnp.arange(FS, dtype=jnp.int32)
    angle = ((cs[:, None] * xs[None, :]) % SG).astype(jnp.float32) * (2.0 * math.pi / SG)
    scale = 1.0 / math.sqrt(SG)
    cosine = jnp.cos(angle) * scale
    sine = jnp.sin(angle) * scale
    return jnp.concatenate(
        [jnp.concatenate([cosine, -sine], 1), jnp.concatenate([sine, cosine], 1)], 0
    )


def body(
    vis_coords,
    vis_values,
    block_dest,
    block_local,
    block_tile,
    block_counts,
    facet_offsets,
    correction,
):
    n_tm = lax.axis_size("tm")
    n_sub = lax.axis_size("sub")
    devices = n_tm * n_sub
    blocks = vis_coords.shape[0]
    band_rows = SG // n_sub
    band_tiles = band_rows // PATCH
    col_tiles = SG // PATCH
    tiles_all = col_tiles * col_tiles
    chunk = SG // devices
    facet_rows = FS // n_sub

    grid = make_phased_grid(
        n_sub,
        vis_coords, vis_values, block_dest, block_tile, block_local, block_counts
    )

    pair = [(i, i ^ 1) for i in range(n_tm)]
    chip_half = grid[: SG // 2] + lax.ppermute(grid[SG // 2 :], "tm", pair)
    half_chunk = chunk // 2
    arrived = lax.all_to_all(
        chip_half.reshape(devices, half_chunk, 2, SG),
        ("tm", "sub"),
        split_axis=0,
        concat_axis=0,
        tiled=True,
    )
    grid_rows = jnp.sum(
        arrived.reshape(n_tm // 2, 2, n_sub, half_chunk, 2, SG), axis=(0, 2)
    )
    grid_rows = (
        grid_rows.reshape(chunk, col_tiles, 2, PATCH).transpose(0, 2, 1, 3).reshape(chunk, 2 * SG)
    )
    offsets = jnp.clip(facet_offsets, 0, SG - FS)
    cs = jnp.arange(SG, dtype=jnp.int32)
    shift = ((offsets[:, 1][:, None] * cs[None, :]) % SG).astype(jnp.float32) * (
        2.0 * math.pi / SG
    )
    cos_s = jnp.cos(shift)[:, None, :]
    sin_s = jnp.sin(shift)[:, None, :]
    g_re = grid_rows[None, :, :SG]
    g_im = grid_rows[None, :, SG:]
    shifted = jnp.concatenate(
        [g_re * cos_s + g_im * sin_s, g_im * cos_s - g_re * sin_s], axis=2
    ).reshape(n_tm * chunk, 2 * SG)
    windows = jnp.dot(shifted, window_table(), precision=lax.Precision.HIGHEST).reshape(
        n_tm, chunk, 2, FS
    )
    windows = jnp.broadcast_to(
        windows[:, None], (n_tm, n_sub, chunk, 2, FS)
    ).reshape(devices, chunk, 2, FS)
    gathered = lax.all_to_all(
        windows, ("tm", "sub"), split_axis=0, concat_axis=0, tiled=True
    ).reshape(SG, 2, FS)

    facet = lax.axis_index("tm")
    band = lax.axis_index("sub")
    first_y = offsets[facet, 0] + band * facet_rows
    ys = first_y + jnp.arange(facet_rows, dtype=jnp.int32)
    order = jnp.arange(SG, dtype=jnp.int32)
    rs = (
        ((order // half_chunk) % 2) * (SG // 2)
        + (order // chunk) * half_chunk
        + order % half_chunk
    )
    angle = ((ys[:, None] * rs[None, :]) % SG).astype(jnp.float32) * (2.0 * math.pi / SG)
    scale = 1.0 / math.sqrt(SG)
    left = jnp.concatenate([jnp.cos(angle) * scale, jnp.sin(angle) * scale], 1)
    real_part = gathered[:, 0]
    imag_part = gathered[:, 1]
    right = jnp.concatenate(
        [
            jnp.concatenate([real_part, imag_part], 1),
            jnp.concatenate([imag_part, -real_part], 1),
        ],
        0,
    )
    summed = jnp.dot(left, right, precision=lax.Precision.HIGHEST).reshape(
        1, facet_rows, 2, FS
    )
    return summed * correction[:, :, None, :]


def solution(mesh):
    in_specs = (
        P(("tm", "sub"), None, None),
        P(("tm", "sub"), None, None),
        P(("tm", "sub"), None),
        P(("tm", "sub")),
        P(("tm", "sub")),
        P(("tm", "sub")),
        P(),
        P("tm", "sub", None),
    )
    out_specs = P("tm", "sub", None, None)
    return jax.shard_map(body, mesh=mesh, in_specs=in_specs, out_specs=out_specs, check_vma=False)
```
